32 devices in a mesh: dp: 4 (over y, x), seq: 8 (over z, core).
Axes of the slice: x: 2, y: 2, z: 4, core: 2. Of those that a mesh axis runs over, the one named last changes fastest.
Arguments:
- hidden_in: bfloat16 [8192, 2048], P(('dp', 'seq')), parts along dimension 0, may hold values from -6 to 6
- lin_query: bfloat16 [8192, 1024], P(('dp', 'seq')), parts along dimension 0, may hold values from -6 to 6
- lin_key: bfloat16 [8192, 256], P(('dp', 'seq')), parts along dimension 0, may hold values from -6 to 6
- lin_value: bfloat16 [8192, 256], P(('dp', 'seq')), parts along dimension 0, may hold values from -6 to 6
- lin_gain: float32 [1024], replicated, may hold values from 0.1 to 1.9
- lin_out_weight: bfloat16 [1024, 2048], replicated, may hold values from -0.1875 to 0.1875
- soft_gain: float32 [2048], replicated, may hold values from 0.1 to 1.9
- soft_wq: bfloat16 [2048, 1024], replicated, may hold values from -4 to 4
- soft_wk: bfloat16 [2048, 256], replicated, may hold values from -4 to 4
- soft_wv: bfloat16 [2048, 256], replicated, may hold values from -0.125 to 0.125
- pattern: int32 [2, 16, 18], replicated, may hold values from 0 to 15, as said below
Outputs:
- attended: bfloat16 [8192, 1024], P(('dp', 'seq')), parts along dimension 0
The draws below stay inside these ranges and needn't reach their ends.
There are 4 independent parts, one for each index of `dp`. The reference program is written for one: setup_inputs(seed, part) draws one part's arguments, and reference() takes and returns one part's arrays. A program takes and returns all parts, laid end to end along the dimension named above; an argument that names none is the same for every part. Nothing has to cross between parts.
Inputs may be any that keep to these rules, and one draw needn't show every extreme that they name: pattern[g, b, 0] = b and pattern[g, b, 1] = max(b - 1, 0); every entry of row b lies between 0 and b; for each key-value head and the 2 query blocks held by one device, the entries in slots 2 to 17 of those rows that lie in another device's tokens all name the same key block of that device.
All inputs are finite; a program needn't handle non-finite values.
Results may differ from the reference program's by a relative error of at most 0.035.
Values may be sent and summed in bfloat16 or wider, within the bound.
No kernel may reach another device: no remote copies, remote signals or barrier semaphores. Data moves between devices by JAX's collectives and lax.ppermute only.
A program may use at most 128 MiB of HBM per device.

```python
import jax
import jax.numpy as jnp
from jax import lax

D = 2048
HEAD_DIM = 128
HEADS = 8
KV_HEADS = 2
BLOCK = 128
SEL = 18
TOK_DEV = 256
TOKENS = 2048
NBLK = 16
Q_DIM = 1024
KV_DIM = 256


def query_base(key):
    return jax.random.normal(jax.random.fold_in(key, 71), (D, HEADS * HEAD_DIM), jnp.float32) * D ** (-0.5)


def draw_soft_wq(key, part):
    return jnp.clip(query_base(key), -4.0, 4.0).astype(jnp.bfloat16)


def draw_soft_wk(key, part):
    noise = jax.random.normal(jax.random.fold_in(key, 72), (D, KV_HEADS * HEAD_DIM), jnp.float32) * D ** (-0.5)
    return jnp.clip(noise, -4.0, 4.0).astype(jnp.bfloat16)


def draw_pattern(key, part):
    per_dev = TOK_DEV // BLOCK
    dev_count = NBLK // per_dev
    far_count = per_dev * (SEL - 2)
    block_ids = jnp.arange(NBLK, dtype=jnp.int32)
    devices = jnp.arange(dev_count, dtype=jnp.int32)
    noise = jax.random.randint(jax.random.fold_in(key, 81), (KV_HEADS, dev_count, dev_count), 0, 1 << 20)
    before = devices[None, None, :] < devices[None, :, None]
    ranking = jnp.where(before, noise, 1 << 20) * dev_count + devices[None, None, :]
    order = jnp.argsort(ranking, axis=-1, stable=True).astype(jnp.int32)
    limits = jnp.maximum(devices, 1)
    slots = jnp.arange(far_count, dtype=jnp.int32)[None, :] % limits[:, None]
    slots = jnp.broadcast_to(slots[None], (KV_HEADS, dev_count, far_count))
    chosen = jnp.take_along_axis(order, slots, axis=-1)
    offsets = jax.random.randint(jax.random.fold_in(key, 82), (KV_HEADS, dev_count), 0, per_dev)
    far_entries = chosen * per_dev + offsets[:, :, None]
    far_entries = far_entries.reshape(KV_HEADS, NBLK, SEL - 2)
    far_entries = jnp.minimum(far_entries, block_ids[None, :, None])
    first = jnp.broadcast_to(block_ids[None, :, None], (KV_HEADS, NBLK, 1))
    second = jnp.broadcast_to(jnp.maximum(block_ids - 1, 0)[None, :, None], (KV_HEADS, NBLK, 1))
    return jnp.concatenate([first, second, far_entries], axis=2).astype(jnp.int32)


def levels(rng, shape, shards, least, high):
    def one(position, parts):
        draws = jax.random.uniform(jax.random.fold_in(jax.random.fold_in(rng, 6), position), (parts,), jnp.float32, least / len(shards), high / len(shards))
        return jnp.repeat(jnp.exp(draws), shape[position] // parts).reshape((-1,) + (1,) * (len(shape) - position - 1))

    gain = one(*shards[0])
    for cut in shards[1:]:
        gain = gain * one(*cut)
    return gain


def bell_draw(stream_key, extent, deviation, limit, pieces=(), held_as=jnp.bfloat16):
    values = deviation * jax.random.normal(stream_key, extent, jnp.float32)
    if pieces:
        values = values * levels(stream_key, extent, pieces, -0.22, 0.18)
    return jnp.clip(values, -limit, limit).astype(held_as)


def setup_inputs(seed: int = 0, part: int = 0) -> dict:
    splits = jax.random.split(jax.random.key(seed), 12)
    part_keys = jax.random.split(jax.random.fold_in(splits[11], part), 12)
    return {
        "hidden_in": bell_draw(part_keys[0], (TOKENS, D), 1.0, 6.0, ((0, 8),)),
        "lin_query": bell_draw(part_keys[1], (TOKENS, Q_DIM), 1.0, 6.0, ((0, 8),)),
        "lin_key": bell_draw(part_keys[2], (TOKENS, KV_DIM), 1.0, 6.0, ((0, 8),)),
        "lin_value": bell_draw(part_keys[3], (TOKENS, KV_DIM), 1.0, 6.0, ((0, 8),)),
        "lin_gain": jnp.clip(1.0 + 0.18 * jax.random.normal(splits[4], (Q_DIM,), jnp.float32), 0.1, 1.9),
        "lin_out_weight": bell_draw(splits[5], (Q_DIM, D), Q_DIM ** -0.5, 0.1875),
        "soft_gain": jnp.clip(1.0 + 0.18 * jax.random.normal(splits[6], (D,), jnp.float32), 0.1, 1.9),
        "soft_wq": draw_soft_wq(jax.random.fold_in(splits[11], 71), part),
        "soft_wk": draw_soft_wk(jax.random.fold_in(splits[11], 71), part),
        "soft_wv": bell_draw(splits[9], (D, KV_DIM), D ** -0.5, 0.125),
        "pattern": draw_pattern(jax.random.fold_in(splits[11], 71), part),
    }


EPSILON = 1e-06

def linear_mixer(lin_query, lin_key, lin_value):
    blocks_total = lin_query.shape[0] // BLOCK
    per_group = HEADS // KV_HEADS
    queries = lin_query.reshape(blocks_total, BLOCK, KV_HEADS, per_group, HEAD_DIM).astype(jnp.float32)
    keys_all = lin_key.reshape(blocks_total, BLOCK, KV_HEADS, HEAD_DIM).astype(jnp.float32)
    values_all = lin_value.reshape(blocks_total, BLOCK, KV_HEADS, HEAD_DIM).astype(jnp.float32)
    positions = jnp.arange(BLOCK)
    causal = positions[:, None] >= positions[None, :]

    def advance(state, inputs):
        query_block, key_block, value_block = inputs
        inter = jnp.einsum('tgpd,gde->tgpe', query_block, state, precision=lax.Precision.HIGHEST)
        scores = jnp.einsum('tgpd,sgd->gpts', query_block, key_block, precision=lax.Precision.HIGHEST)
        scores = jnp.where(causal, scores, 0.0)
        rounded = lax.optimization_barrier(scores.astype(jnp.bfloat16)).astype(jnp.float32)
        intra = jnp.einsum('gpts,sge->tgpe', rounded, value_block, precision=lax.Precision.HIGHEST)
        updated = state + jnp.einsum('tgd,tge->gde', key_block, value_block, precision=lax.Precision.HIGHEST)
        return (updated, inter + intra)
    start = jnp.zeros((KV_HEADS, HEAD_DIM, HEAD_DIM), jnp.float32)
    final_state, mixed = lax.scan(advance, start, (queries, keys_all, values_all))
    return mixed.reshape(-1, HEADS, HEAD_DIM)

def sparse_attention(soft_query, packed, pattern):
    blocks_total = packed.shape[0] // BLOCK
    per_group = HEADS // KV_HEADS
    listed = pattern.shape[2]
    table = packed.reshape(blocks_total, BLOCK, KV_HEADS, 2 * HEAD_DIM)
    queries = soft_query.reshape(blocks_total, BLOCK, KV_HEADS, per_group, HEAD_DIM)
    group_ids = jnp.arange(KV_HEADS)[:, None]
    rows_here = jnp.arange(BLOCK)
    columns = jnp.arange(listed * BLOCK)
    causal = (columns[None, :] >= BLOCK) | (columns[None, :] <= rows_here[:, None])
    earlier = jnp.arange(listed)[None, :] < jnp.arange(listed)[:, None]
    scale = HEAD_DIM ** (-0.5)

    def one_block(inputs):
        query_block, entries = inputs
        tiles = table[entries, :, group_ids, :]
        tiles = tiles.reshape(KV_HEADS, listed * BLOCK, 2 * HEAD_DIM).astype(jnp.float32)
        keys_tile = tiles[:, :, :HEAD_DIM]
        values_tile = tiles[:, :, HEAD_DIM:]
        same = entries[:, :, None] == entries[:, None, :]
        repeated = jnp.any(same & earlier[None], axis=-1)
        live = jnp.repeat(jnp.logical_not(repeated), BLOCK, axis=-1)
        allowed = live[:, None, None, :] & causal[None, None]
        scores = jnp.einsum('tgpd,gkd->gptk', query_block.astype(jnp.float32), keys_tile, precision=lax.Precision.HIGHEST) * scale
        highest = lax.optimization_barrier(jnp.max(jnp.where(allowed, scores, -jnp.inf), axis=-1, keepdims=True))
        weights = jnp.where(allowed, jnp.exp(scores - highest), 0.0)
        total = lax.optimization_barrier(jnp.sum(weights, axis=-1, keepdims=True))
        probs = lax.optimization_barrier((weights / total).astype(jnp.bfloat16)).astype(jnp.float32)
        result = jnp.einsum('gptk,gke->tgpe', probs, values_tile, precision=lax.Precision.HIGHEST)
        return result.reshape(BLOCK, HEADS * HEAD_DIM).astype(jnp.bfloat16)
    outputs = lax.map(one_block, (queries, jnp.transpose(pattern, (1, 0, 2))))
    return outputs.reshape(-1, HEADS * HEAD_DIM)

def reference(hidden_in, lin_query, lin_key, lin_value, lin_gain, lin_out_weight, soft_gain, soft_wq, soft_wk, soft_wv, pattern):
    mixed = linear_mixer(lin_query, lin_key, lin_value)
    normed = mixed * lax.rsqrt(lax.optimization_barrier(jnp.mean(mixed * mixed, axis=-1, keepdims=True)) + EPSILON) * lin_gain.reshape(HEADS, HEAD_DIM)
    normed = normed.reshape(-1, HEADS * HEAD_DIM).astype(jnp.bfloat16)
    branch = jnp.dot(normed, lin_out_weight, preferred_element_type=jnp.float32)
    residual = (hidden_in.astype(jnp.float32) + branch).astype(jnp.bfloat16)
    widened = lax.optimization_barrier(residual).astype(jnp.float32)
    layer_in = (widened * lax.rsqrt(lax.optimization_barrier(jnp.mean(widened * widened, axis=-1, keepdims=True)) + EPSILON) * soft_gain).astype(jnp.bfloat16)
    soft_query = jnp.dot(layer_in, soft_wq, preferred_element_type=jnp.float32).astype(jnp.bfloat16)
    soft_key = jnp.dot(layer_in, soft_wk, preferred_element_type=jnp.float32).astype(jnp.bfloat16)
    soft_value = jnp.dot(layer_in, soft_wv, preferred_element_type=jnp.float32).astype(jnp.bfloat16)
    packed = jnp.concatenate([soft_key.reshape(-1, KV_HEADS, HEAD_DIM), soft_value.reshape(-1, KV_HEADS, HEAD_DIM)], axis=-1)
    return sparse_attention(soft_query, packed, pattern)
```

```python
import functools

import jax
import jax.numpy as jnp
from jax import lax
from jax.experimental import pallas as pl
from jax.experimental.pallas import tpu as pltpu
from jax.sharding import PartitionSpec as P

HEAD_DIM = 128
HEADS = 8
KV_HEADS = 2
BLOCK = 128
DENSE_MAX_BLOCKS = 32


EPSILON = 1e-06


def exclusive_prefix(state, axis, devices):
    total = jnp.zeros_like(state)
    window = state
    shift = 1
    while shift < devices:
        pairs = [(i, i + shift) for i in range(devices - shift)]
        got = lax.ppermute(window, axis, pairs)
        total = total + got
        if shift * 2 < devices:
            window = window + got
        shift *= 2
    return total


def attention_kernel(q_ref, kv_ref, code_ref, o_ref, *, per_group):
    keys_total = kv_ref.shape[0]
    keys = kv_ref[:, :HEAD_DIM]
    values = kv_ref[:, HEAD_DIM:]
    code = code_ref[...]
    rows = lax.broadcasted_iota(jnp.int32, (BLOCK, keys_total), 0)
    cols = lax.broadcasted_iota(jnp.int32, (BLOCK, keys_total), 1)
    cols = jnp.bitwise_and(cols, BLOCK - 1)
    allowed = (code == 1) | ((code == 2) & (cols <= rows))
    scale = HEAD_DIM ** (-0.5)
    for p in range(per_group):
        qp = q_ref[:, p * HEAD_DIM:(p + 1) * HEAD_DIM]
        scores = lax.dot_general(
            qp, keys, (((1,), (1,)), ((), ())), preferred_element_type=jnp.float32
        ) * scale
        scores = jnp.where(allowed, scores, -jnp.inf)
        highest = jnp.max(scores, axis=-1, keepdims=True)
        weights = jnp.where(allowed, jnp.exp(scores - highest), 0.0)
        total = jnp.sum(weights, axis=-1, keepdims=True)
        probs = (weights * (1.0 / total)).astype(jnp.bfloat16)
        out = jnp.dot(probs, values, preferred_element_type=jnp.float32)
        o_ref[:, p * HEAD_DIM:(p + 1) * HEAD_DIM] = out.astype(o_ref.dtype)


def attention(soft_query, kv, code, dense):
    tok_count = soft_query.shape[0]
    local_blocks = tok_count // BLOCK
    per_group = HEADS // KV_HEADS
    keys_total = code.shape[-1]
    width = per_group * HEAD_DIM
    if dense:
        kv_spec = pl.BlockSpec((keys_total, 2 * HEAD_DIM), lambda g, n: (0, g))
    else:
        kv_spec = pl.BlockSpec((None, None, keys_total, 2 * HEAD_DIM), lambda g, n: (g, n, 0, 0))
    flops = 4 * tok_count * HEADS * keys_total * HEAD_DIM
    bytes_accessed = 2 * (2 * soft_query.size + KV_HEADS * local_blocks * keys_total * 2 * HEAD_DIM)
    return pl.pallas_call(
        functools.partial(attention_kernel, per_group=per_group),
        out_shape=jax.ShapeDtypeStruct(soft_query.shape, jnp.bfloat16),
        grid=(KV_HEADS, local_blocks),
        in_specs=[
            pl.BlockSpec((BLOCK, width), lambda g, n: (n, g)),
            kv_spec,
            pl.BlockSpec((None, None, 1, keys_total), lambda g, n: (g, n, 0, 0)),
        ],
        out_specs=pl.BlockSpec((BLOCK, width), lambda g, n: (n, g)),
        compiler_params=pltpu.CompilerParams(vmem_limit_bytes=48 * 1024 * 1024),
        cost_estimate=pl.CostEstimate(
            flops=flops, transcendentals=tok_count * HEADS * keys_total, bytes_accessed=bytes_accessed
        ),
    )(soft_query, kv, code)


def local(
    hidden_in,
    lin_query,
    lin_key,
    lin_value,
    lin_gain,
    lin_out_weight,
    soft_gain,
    soft_wq,
    soft_wk,
    soft_wv,
    pattern,
    *,
    devices,
):
    tok_count = hidden_in.shape[0]
    local_blocks = tok_count // BLOCK
    per_group = HEADS // KV_HEADS
    listed = pattern.shape[2]
    position = lax.axis_index("seq")
    query_blocks = lin_query.reshape(local_blocks, BLOCK, KV_HEADS, per_group, HEAD_DIM)
    key_blocks = lin_key.reshape(local_blocks, BLOCK, KV_HEADS, HEAD_DIM)
    value_blocks = lin_value.reshape(local_blocks, BLOCK, KV_HEADS, HEAD_DIM)
    block_states = jnp.einsum(
        "ntgd,ntge->ngde", key_blocks, value_blocks, preferred_element_type=jnp.float32
    )
    device_state = jnp.sum(block_states, axis=0)
    carried = exclusive_prefix(device_state, "seq", devices)
    running = jnp.concatenate(
        [jnp.zeros_like(block_states[:1]), jnp.cumsum(block_states[:-1], axis=0)], axis=0
    )
    before = carried[None] + running
    inter = jnp.einsum(
        "ntgpd,ngde->ntgpe",
        query_blocks.astype(jnp.float32),
        before,
        precision=lax.Precision.HIGHEST,
    )
    rows_here = jnp.arange(BLOCK)
    causal = rows_here[:, None] >= rows_here[None, :]
    local_scores = jnp.einsum(
        "ntgpd,nsgd->ngpts", query_blocks, key_blocks, preferred_element_type=jnp.float32
    )
    local_scores = jnp.where(causal, local_scores, 0.0).astype(jnp.bfloat16)
    intra = jnp.einsum(
        "ngpts,nsge->ntgpe", local_scores, value_blocks, preferred_element_type=jnp.float32
    )
    mixed = (inter + intra).reshape(tok_count, HEADS, HEAD_DIM)
    normed = (
        mixed
        * lax.rsqrt(jnp.mean(mixed * mixed, axis=-1, keepdims=True) + EPSILON)
        * lin_gain.reshape(HEADS, HEAD_DIM)
    )
    normed = normed.reshape(tok_count, HEADS * HEAD_DIM).astype(jnp.bfloat16)
    branch = jnp.dot(normed, lin_out_weight, preferred_element_type=jnp.float32)
    residual = (hidden_in.astype(jnp.float32) + branch).astype(jnp.bfloat16)
    widened = residual.astype(jnp.float32)
    layer_in = (
        widened
        * lax.rsqrt(jnp.mean(widened * widened, axis=-1, keepdims=True) + EPSILON)
        * soft_gain
    ).astype(jnp.bfloat16)
    soft_key = jnp.dot(layer_in, soft_wk, preferred_element_type=jnp.float32).astype(jnp.bfloat16)
    soft_value = jnp.dot(layer_in, soft_wv, preferred_element_type=jnp.float32).astype(jnp.bfloat16)
    packed = jnp.concatenate(
        [
            soft_key.reshape(tok_count, KV_HEADS, HEAD_DIM),
            soft_value.reshape(tok_count, KV_HEADS, HEAD_DIM),
        ],
        axis=-1,
    )
    whole = lax.all_gather(packed, "seq", axis=0, tiled=True)
    soft_query = jnp.dot(layer_in, soft_wq, preferred_element_type=jnp.float32).astype(jnp.bfloat16)

    mine = lax.dynamic_slice_in_dim(pattern, position * local_blocks, local_blocks, 1)
    total_blocks = devices * local_blocks
    dense = total_blocks <= DENSE_MAX_BLOCKS
    if dense:
        block_ids = jnp.arange(total_blocks, dtype=jnp.int32)
        present = jnp.any(mine[..., :, None] == block_ids, axis=-2)
        own = mine[..., :1] == block_ids
        code = jnp.where(own, 2, present.astype(jnp.int32))
        kv = whole.reshape(total_blocks * BLOCK, KV_HEADS * 2 * HEAD_DIM)
    else:
        same = mine[..., :, None] == mine[..., None, :]
        earlier = jnp.arange(listed)[None, :] < jnp.arange(listed)[:, None]
        repeated = jnp.any(same & earlier, axis=-1)
        first_slot = (jnp.arange(listed) == 0)[None, None, :]
        code = jnp.where(first_slot, 2, jnp.logical_not(repeated).astype(jnp.int32))
        table = whole.reshape(-1, BLOCK, KV_HEADS, 2 * HEAD_DIM)
        group_ids = jnp.arange(KV_HEADS)[:, None, None]
        tiles = table[mine, :, group_ids, :]
        kv = tiles.reshape(KV_HEADS, local_blocks, listed * BLOCK, 2 * HEAD_DIM)
    code = jnp.repeat(code, BLOCK, axis=-1)[:, :, None, :]
    return attention(soft_query, kv, code, dense)


def solution(mesh):
    in_specs = (
        P(("dp", "seq"), None),
        P(("dp", "seq"), None),
        P(("dp", "seq"), None),
        P(("dp", "seq"), None),
        P(),
        P(),
        P(),
        P(),
        P(),
        P(),
        P(),
    )
    out_specs = P(("dp", "seq"), None)
    body = functools.partial(local, devices=mesh.shape["seq"])
    return jax.shard_map(body, mesh=mesh, in_specs=in_specs, out_specs=out_specs, check_vma=False)
```

```python
import functools

import jax
import jax.numpy as jnp
from jax import lax
from jax.experimental import pallas as pl
from jax.experimental.pallas import tpu as pltpu
from jax.sharding import PartitionSpec as P

HEAD_DIM = 128
HEADS = 8
KV_HEADS = 2
BLOCK = 128
EXCHANGE_MAX_DEVICES = 16


EPSILON = 1e-06


def exclusive_prefix(state, axis, devices):
    total = jnp.zeros_like(state)
    window = state
    shift = 1
    while shift < devices:
        pairs = [(i, i + shift) for i in range(devices - shift)]
        got = lax.ppermute(window, axis, pairs)
        total = total + got
        if shift * 2 < devices:
            window = window + got
        shift *= 2
    return total


def attention_kernel(q_ref, kv_ref, code_ref, o_ref, *, per_group):
    keys_total = kv_ref.shape[0]
    keys = kv_ref[:, :HEAD_DIM]
    values = kv_ref[:, HEAD_DIM:]
    code = code_ref[...]
    rows = lax.broadcasted_iota(jnp.int32, (BLOCK, keys_total), 0)
    cols = lax.broadcasted_iota(jnp.int32, (BLOCK, keys_total), 1)
    cols = jnp.bitwise_and(cols, BLOCK - 1)
    allowed = (code == 1) | ((code == 2) & (cols <= rows))
    scale = HEAD_DIM ** (-0.5)
    for p in range(per_group):
        qp = q_ref[:, p * HEAD_DIM:(p + 1) * HEAD_DIM]
        scores = lax.dot_general(
            qp, keys, (((1,), (1,)), ((), ())), preferred_element_type=jnp.float32
        ) * scale
        scores = jnp.where(allowed, scores, -jnp.inf)
        highest = jnp.max(scores, axis=-1, keepdims=True)
        weights = jnp.where(allowed, jnp.exp(scores - highest), 0.0)
        total = jnp.sum(weights, axis=-1, keepdims=True)
        probs = (weights * (1.0 / total)).astype(jnp.bfloat16)
        out = jnp.dot(probs, values, preferred_element_type=jnp.float32)
        o_ref[:, p * HEAD_DIM:(p + 1) * HEAD_DIM] = out.astype(o_ref.dtype)


def attention(soft_query, kv, code):
    tok_count = soft_query.shape[0]
    local_blocks = tok_count // BLOCK
    per_group = HEADS // KV_HEADS
    keys_total = code.shape[-1]
    width = per_group * HEAD_DIM
    if kv.ndim == 3:
        kv_spec = pl.BlockSpec((None, keys_total, 2 * HEAD_DIM), lambda g, n: (g, 0, 0))
    else:
        kv_spec = pl.BlockSpec((None, None, keys_total, 2 * HEAD_DIM), lambda g, n: (g, n, 0, 0))
    flops = 4 * tok_count * HEADS * keys_total * HEAD_DIM
    bytes_accessed = 2 * (2 * soft_query.size + KV_HEADS * local_blocks * keys_total * 2 * HEAD_DIM)
    return pl.pallas_call(
        functools.partial(attention_kernel, per_group=per_group),
        out_shape=jax.ShapeDtypeStruct(soft_query.shape, jnp.bfloat16),
        grid=(KV_HEADS, local_blocks),
        in_specs=[
            pl.BlockSpec((BLOCK, width), lambda g, n: (n, g)),
            kv_spec,
            pl.BlockSpec((None, None, 1, keys_total), lambda g, n: (g, n, 0, 0)),
        ],
        out_specs=pl.BlockSpec((BLOCK, width), lambda g, n: (n, g)),
        compiler_params=pltpu.CompilerParams(vmem_limit_bytes=48 * 1024 * 1024),
        cost_estimate=pl.CostEstimate(
            flops=flops, transcendentals=tok_count * HEADS * keys_total, bytes_accessed=bytes_accessed
        ),
    )(soft_query, kv, code)


def exchange_kv(packed, pattern, position, devices):
    tok_count = packed.shape[0]
    local_blocks = tok_count // BLOCK
    blocks = packed.reshape(local_blocks, BLOCK, KV_HEADS, 2 * HEAD_DIM)
    heads = jnp.arange(KV_HEADS)
    per_head = jnp.transpose(blocks, (2, 0, 1, 3)).reshape(KV_HEADS, tok_count, 2 * HEAD_DIM)
    pieces = [per_head]
    own_ids = position * local_blocks + jnp.arange(local_blocks, dtype=jnp.int32)
    ids = [jnp.broadcast_to(own_ids, (KV_HEADS, local_blocks))]
    if devices > 1:
        pairs = [(i, i + 1) for i in range(devices - 1)]
        pieces.append(lax.ppermute(per_head, "seq", pairs))
        near = own_ids - local_blocks
        ids.append(jnp.broadcast_to(jnp.where(position >= 1, near, -1), (KV_HEADS, local_blocks)))
    mine = lax.dynamic_slice_in_dim(pattern, position * local_blocks, local_blocks, 1)
    my_far = mine[:, :, 2:].reshape(KV_HEADS, -1)
    for shift in range(2, devices):
        dest = jnp.minimum(position + shift, devices - 1)
        rows = lax.dynamic_slice_in_dim(pattern, dest * local_blocks, local_blocks, 1)
        far = rows[:, :, 2:].reshape(KV_HEADS, -1)
        on_me = (far // local_blocks) == position
        choice = jnp.max(jnp.where(on_me, far - position * local_blocks, 0), axis=-1)
        chosen = blocks[choice, :, heads, :]
        pairs = [(i, i + shift) for i in range(devices - shift)]
        pieces.append(lax.ppermute(chosen, "seq", pairs))
        source = position - shift
        on_src = (my_far // local_blocks) == source
        got_id = jnp.max(jnp.where(on_src, my_far, -1), axis=-1)
        ids.append(jnp.where(source >= 0, got_id, -1)[:, None])
    table = jnp.concatenate(pieces, axis=1)
    slot_ids = jnp.concatenate(ids, axis=1)
    present = jnp.any(mine[:, :, :, None] == slot_ids[:, None, None, :], axis=2)
    present = present & (slot_ids >= 0)[:, None, :]
    own = mine[:, :, :1] == slot_ids[:, None, :]
    code = jnp.where(own, 2, present.astype(jnp.int32))
    return table, code


def local(
    hidden_in,
    lin_query,
    lin_key,
    lin_value,
    lin_gain,
    lin_out_weight,
    soft_gain,
    soft_wq,
    soft_wk,
    soft_wv,
    pattern,
    *,
    devices,
):
    tok_count = hidden_in.shape[0]
    local_blocks = tok_count // BLOCK
    per_group = HEADS // KV_HEADS
    listed = pattern.shape[2]
    position = lax.axis_index("seq")
    query_blocks = lin_query.reshape(local_blocks, BLOCK, KV_HEADS, per_group, HEAD_DIM)
    key_blocks = lin_key.reshape(local_blocks, BLOCK, KV_HEADS, HEAD_DIM)
    value_blocks = lin_value.reshape(local_blocks, BLOCK, KV_HEADS, HEAD_DIM)
    block_states = jnp.einsum(
        "ntgd,ntge->ngde", key_blocks, value_blocks, preferred_element_type=jnp.float32
    )
    device_state = jnp.sum(block_states, axis=0)
    carried = exclusive_prefix(device_state, "seq", devices)
    running = jnp.concatenate(
        [jnp.zeros_like(block_states[:1]), jnp.cumsum(block_states[:-1], axis=0)], axis=0
    )
    before = carried[None] + running
    inter = jnp.einsum(
        "ntgpd,ngde->ntgpe",
        query_blocks.astype(jnp.float32),
        before,
        precision=lax.Precision.HIGHEST,
    )
    rows_here = jnp.arange(BLOCK)
    causal = rows_here[:, None] >= rows_here[None, :]
    local_scores = jnp.einsum(
        "ntgpd,nsgd->ngpts", query_blocks, key_blocks, preferred_element_type=jnp.float32
    )
    local_scores = jnp.where(causal, local_scores, 0.0).astype(jnp.bfloat16)
    intra = jnp.einsum(
        "ngpts,nsge->ntgpe", local_scores, value_blocks, preferred_element_type=jnp.float32
    )
    mixed = (inter + intra).reshape(tok_count, HEADS, HEAD_DIM)
    normed = (
        mixed
        * lax.rsqrt(jnp.mean(mixed * mixed, axis=-1, keepdims=True) + EPSILON)
        * lin_gain.reshape(HEADS, HEAD_DIM)
    )
    normed = normed.reshape(tok_count, HEADS * HEAD_DIM).astype(jnp.bfloat16)
    branch = jnp.dot(normed, lin_out_weight, preferred_element_type=jnp.float32)
    residual = (hidden_in.astype(jnp.float32) + branch).astype(jnp.bfloat16)
    widened = residual.astype(jnp.float32)
    layer_in = (
        widened
        * lax.rsqrt(jnp.mean(widened * widened, axis=-1, keepdims=True) + EPSILON)
        * soft_gain
    ).astype(jnp.bfloat16)
    soft_key = jnp.dot(layer_in, soft_wk, preferred_element_type=jnp.float32).astype(jnp.bfloat16)
    soft_value = jnp.dot(layer_in, soft_wv, preferred_element_type=jnp.float32).astype(jnp.bfloat16)
    packed = jnp.concatenate(
        [
            soft_key.reshape(tok_count, KV_HEADS, HEAD_DIM),
            soft_value.reshape(tok_count, KV_HEADS, HEAD_DIM),
        ],
        axis=-1,
    )
    soft_query = jnp.dot(layer_in, soft_wq, preferred_element_type=jnp.float32).astype(jnp.bfloat16)

    if devices <= EXCHANGE_MAX_DEVICES:
        kv, code = exchange_kv(packed, pattern, position, devices)
    else:
        whole = lax.all_gather(packed, "seq", axis=0, tiled=True)
        mine = lax.dynamic_slice_in_dim(pattern, position * local_blocks, local_blocks, 1)
        same = mine[..., :, None] == mine[..., None, :]
        earlier = jnp.arange(listed)[None, :] < jnp.arange(listed)[:, None]
        repeated = jnp.any(same & earlier, axis=-1)
        first_slot = (jnp.arange(listed) == 0)[None, None, :]
        code = jnp.where(first_slot, 2, jnp.logical_not(repeated).astype(jnp.int32))
        table = whole.reshape(-1, BLOCK, KV_HEADS, 2 * HEAD_DIM)
        group_ids = jnp.arange(KV_HEADS)[:, None, None]
        tiles = table[mine, :, group_ids, :]
        kv = tiles.reshape(KV_HEADS, local_blocks, listed * BLOCK, 2 * HEAD_DIM)
    code = jnp.repeat(code, BLOCK, axis=-1)[:, :, None, :]
    return attention(soft_query, kv, code)


def solution(mesh):
    in_specs = (
        P(("dp", "seq"), None),
        P(("dp", "seq"), None),
        P(("dp", "seq"), None),
        P(("dp", "seq"), None),
        P(),
        P(),
        P(),
        P(),
        P(),
        P(),
        P(),
    )
    out_specs = P(("dp", "seq"), None)
    body = functools.partial(local, devices=mesh.shape["seq"])
    return jax.shard_map(body, mesh=mesh, in_specs=in_specs, out_specs=out_specs, check_vma=False)
```

```python
import functools

import jax
import jax.numpy as jnp
from jax import lax
from jax.experimental import pallas as pl
from jax.experimental.pallas import tpu as pltpu
from jax.sharding import PartitionSpec as P

HEAD_DIM = 128
HEADS = 8
KV_HEADS = 2
BLOCK = 128
EXCHANGE_MAX_DEVICES = 16


EPSILON = 1e-06


def exclusive_prefix(state, axis, devices):
    total = jnp.zeros_like(state)
    window = state
    shift = 1
    while shift < devices:
        pairs = [(i, i + shift) for i in range(devices - shift)]
        got = lax.ppermute(window, axis, pairs)
        total = total + got
        if shift * 2 < devices:
            window = window + got
        shift *= 2
    return total


def attention_kernel(q_ref, *refs, per_group, kv_count):
    kv_refs = refs[:kv_count]
    code_ref = refs[kv_count]
    o_ref = refs[kv_count + 1]
    chunks = []
    for ref in kv_refs:
        for start in range(0, ref.shape[0], BLOCK):
            chunks.append((ref, start))
    code = code_ref[...]
    rows = lax.broadcasted_iota(jnp.int32, (BLOCK, BLOCK), 0)
    cols = lax.broadcasted_iota(jnp.int32, (BLOCK, BLOCK), 1)
    lower = cols <= rows
    masks = []
    for c in range(len(chunks)):
        part = code[:, c * BLOCK:(c + 1) * BLOCK]
        masks.append((part == 1) | ((part == 2) & lower))
    scale = HEAD_DIM ** (-0.5)
    for p in range(per_group):
        qp = q_ref[:, p * HEAD_DIM:(p + 1) * HEAD_DIM]
        scores = []
        for (ref, start), allowed in zip(chunks, masks):
            keys = ref[start:start + BLOCK, :HEAD_DIM]
            s = lax.dot_general(
                qp, keys, (((1,), (1,)), ((), ())), preferred_element_type=jnp.float32
            ) * scale
            scores.append(jnp.where(allowed, s, -jnp.inf))
        highest = scores[0].max(axis=-1, keepdims=True)
        for s in scores[1:]:
            highest = jnp.maximum(highest, s.max(axis=-1, keepdims=True))
        weights = [jnp.where(allowed, jnp.exp(s - highest), 0.0) for s, allowed in zip(scores, masks)]
        total = weights[0].sum(axis=-1, keepdims=True)
        for w in weights[1:]:
            total = total + w.sum(axis=-1, keepdims=True)
        inverse = 1.0 / total
        out = None
        for (ref, start), w in zip(chunks, weights):
            probs = (w * inverse).astype(jnp.bfloat16)
            values = ref[start:start + BLOCK, HEAD_DIM:]
            term = jnp.dot(probs, values, preferred_element_type=jnp.float32)
            out = term if out is None else out + term
        o_ref[:, p * HEAD_DIM:(p + 1) * HEAD_DIM] = out.astype(o_ref.dtype)


def kv_spec(piece):
    if piece.ndim == 3:
        return pl.BlockSpec((None, piece.shape[1], 2 * HEAD_DIM), lambda g, n: (g, 0, 0))
    return pl.BlockSpec((None, None, piece.shape[2], 2 * HEAD_DIM), lambda g, n: (g, n, 0, 0))


def attention(soft_query, pieces, code):
    tok_count = soft_query.shape[0]
    local_blocks = tok_count // BLOCK
    per_group = HEADS // KV_HEADS
    keys_total = code.shape[-1]
    width = per_group * HEAD_DIM
    flops = 4 * tok_count * HEADS * keys_total * HEAD_DIM
    bytes_accessed = 2 * (2 * soft_query.size + KV_HEADS * local_blocks * keys_total * 2 * HEAD_DIM)
    return pl.pallas_call(
        functools.partial(attention_kernel, per_group=per_group, kv_count=len(pieces)),
        out_shape=jax.ShapeDtypeStruct(soft_query.shape, jnp.bfloat16),
        grid=(KV_HEADS, local_blocks),
        in_specs=[pl.BlockSpec((BLOCK, width), lambda g, n: (n, g))]
        + [kv_spec(piece) for piece in pieces]
        + [pl.BlockSpec((None, None, 1, keys_total), lambda g, n: (g, n, 0, 0))],
        out_specs=pl.BlockSpec((BLOCK, width), lambda g, n: (n, g)),
        compiler_params=pltpu.CompilerParams(vmem_limit_bytes=48 * 1024 * 1024),
        cost_estimate=pl.CostEstimate(
            flops=flops, transcendentals=tok_count * HEADS * keys_total, bytes_accessed=bytes_accessed
        ),
    )(soft_query, *pieces, code)


def exchange_kv(packed, pattern, position, devices):
    tok_count = packed.shape[0]
    local_blocks = tok_count // BLOCK
    blocks = packed.reshape(local_blocks, BLOCK, KV_HEADS, 2 * HEAD_DIM)
    per_head = jnp.transpose(blocks, (2, 0, 1, 3)).reshape(KV_HEADS, tok_count, 2 * HEAD_DIM)
    pieces = [per_head]
    own_ids = position * local_blocks + jnp.arange(local_blocks, dtype=jnp.int32)
    ids = [jnp.broadcast_to(own_ids, (KV_HEADS, local_blocks))]
    if devices > 1:
        pairs = [(i, i + 1) for i in range(devices - 1)]
        pieces.append(lax.ppermute(per_head, "seq", pairs))
        near = own_ids - local_blocks
        ids.append(jnp.broadcast_to(jnp.where(position >= 1, near, -1), (KV_HEADS, local_blocks)))
    mine = lax.dynamic_slice_in_dim(pattern, position * local_blocks, local_blocks, 1)
    my_far = mine[:, :, 2:].reshape(KV_HEADS, -1)
    shifts = list(range(2, devices))
    if shifts:
        dests = jnp.minimum(position + jnp.array(shifts, jnp.int32), devices - 1)
        firsts = dests * local_blocks
        rows = jnp.stack(
            [lax.dynamic_slice_in_dim(pattern, firsts[i], local_blocks, 1) for i in range(len(shifts))]
        )
        far = rows[:, :, :, 2:].reshape(len(shifts), KV_HEADS, -1)
        on_me = (far // local_blocks) == position
        choice = jnp.max(jnp.where(on_me, far - position * local_blocks, 0), axis=-1)
        split = per_head.reshape(KV_HEADS, local_blocks, BLOCK, 2 * HEAD_DIM)
        chosen = split[None, :, 0]
        for j in range(1, local_blocks):
            chosen = jnp.where((choice == j)[:, :, None, None], split[None, :, j], chosen)
    for i, shift in enumerate(shifts):
        pairs = [(k, k + shift) for k in range(devices - shift)]
        pieces.append(lax.ppermute(chosen[i], "seq", pairs))
        source = position - shift
        on_src = (my_far // local_blocks) == source
        got_id = jnp.max(jnp.where(on_src, my_far, -1), axis=-1)
        ids.append(jnp.where(source >= 0, got_id, -1)[:, None])
    slot_ids = jnp.concatenate(ids, axis=1)
    present = jnp.any(mine[:, :, :, None] == slot_ids[:, None, None, :], axis=2)
    present = present & (slot_ids >= 0)[:, None, :]
    own = mine[:, :, :1] == slot_ids[:, None, :]
    code = jnp.where(own, 2, present.astype(jnp.int32))
    return pieces, code


def local(
    hidden_in,
    lin_query,
    lin_key,
    lin_value,
    lin_gain,
    lin_out_weight,
    soft_gain,
    soft_wq,
    soft_wk,
    soft_wv,
    pattern,
    *,
    devices,
):
    tok_count = hidden_in.shape[0]
    local_blocks = tok_count // BLOCK
    per_group = HEADS // KV_HEADS
    listed = pattern.shape[2]
    position = lax.axis_index("seq")
    query_blocks = lin_query.reshape(local_blocks, BLOCK, KV_HEADS, per_group, HEAD_DIM)
    key_blocks = lin_key.reshape(local_blocks, BLOCK, KV_HEADS, HEAD_DIM)
    value_blocks = lin_value.reshape(local_blocks, BLOCK, KV_HEADS, HEAD_DIM)
    block_states = jnp.einsum(
        "ntgd,ntge->ngde", key_blocks, value_blocks, preferred_element_type=jnp.float32
    )
    device_state = jnp.sum(block_states, axis=0)
    carried = exclusive_prefix(device_state, "seq", devices)
    running = jnp.concatenate(
        [jnp.zeros_like(block_states[:1]), jnp.cumsum(block_states[:-1], axis=0)], axis=0
    )
    before = carried[None] + running
    inter = jnp.einsum(
        "ntgpd,ngde->ntgpe",
        query_blocks.astype(jnp.float32),
        before,
        precision=lax.Precision.HIGHEST,
    )
    rows_here = jnp.arange(BLOCK)
    causal = rows_here[:, None] >= rows_here[None, :]
    local_scores = jnp.einsum(
        "ntgpd,nsgd->ngpts", query_blocks, key_blocks, preferred_element_type=jnp.float32
    )
    local_scores = jnp.where(causal, local_scores, 0.0).astype(jnp.bfloat16)
    intra = jnp.einsum(
        "ngpts,nsge->ntgpe", local_scores, value_blocks, preferred_element_type=jnp.float32
    )
    mixed = (inter + intra).reshape(tok_count, HEADS, HEAD_DIM)
    normed = (
        mixed
        * lax.rsqrt(jnp.mean(mixed * mixed, axis=-1, keepdims=True) + EPSILON)
        * lin_gain.reshape(HEADS, HEAD_DIM)
    )
    normed = normed.reshape(tok_count, HEADS * HEAD_DIM).astype(jnp.bfloat16)
    branch = jnp.dot(normed, lin_out_weight, preferred_element_type=jnp.float32)
    residual = (hidden_in.astype(jnp.float32) + branch).astype(jnp.bfloat16)
    widened = residual.astype(jnp.float32)
    layer_in = (
        widened
        * lax.rsqrt(jnp.mean(widened * widened, axis=-1, keepdims=True) + EPSILON)
        * soft_gain
    ).astype(jnp.bfloat16)
    soft_key = jnp.dot(layer_in, soft_wk, preferred_element_type=jnp.float32).astype(jnp.bfloat16)
    soft_value = jnp.dot(layer_in, soft_wv, preferred_element_type=jnp.float32).astype(jnp.bfloat16)
    packed = jnp.concatenate(
        [
            soft_key.reshape(tok_count, KV_HEADS, HEAD_DIM),
            soft_value.reshape(tok_count, KV_HEADS, HEAD_DIM),
        ],
        axis=-1,
    )
    soft_query = jnp.dot(layer_in, soft_wq, preferred_element_type=jnp.float32).astype(jnp.bfloat16)

    if devices <= EXCHANGE_MAX_DEVICES:
        pieces, code = exchange_kv(packed, pattern, position, devices)
    else:
        whole = lax.all_gather(packed, "seq", axis=0, tiled=True)
        mine = lax.dynamic_slice_in_dim(pattern, position * local_blocks, local_blocks, 1)
        same = mine[..., :, None] == mine[..., None, :]
        earlier = jnp.arange(listed)[None, :] < jnp.arange(listed)[:, None]
        repeated = jnp.any(same & earlier, axis=-1)
        first_slot = (jnp.arange(listed) == 0)[None, None, :]
        code = jnp.where(first_slot, 2, jnp.logical_not(repeated).astype(jnp.int32))
        table = whole.reshape(-1, BLOCK, KV_HEADS, 2 * HEAD_DIM)
        group_ids = jnp.arange(KV_HEADS)[:, None, None]
        tiles = table[mine, :, group_ids, :]
        pieces = [tiles.reshape(KV_HEADS, local_blocks, listed * BLOCK, 2 * HEAD_DIM)]
    code = jnp.repeat(code, BLOCK, axis=-1)[:, :, None, :]
    return attention(soft_query, pieces, code)


def solution(mesh):
    in_specs = (
        P(("dp", "seq"), None),
        P(("dp", "seq"), None),
        P(("dp", "seq"), None),
        P(("dp", "seq"), None),
        P(),
        P(),
        P(),
        P(),
        P(),
        P(),
        P(),
    )
    out_specs = P(("dp", "seq"), None)
    body = functools.partial(local, devices=mesh.shape["seq"])
    return jax.shard_map(body, mesh=mesh, in_specs=in_specs, out_specs=out_specs, check_vma=False)
```

```python
import functools

import jax
import jax.numpy as jnp
from jax import lax
from jax.experimental import pallas as pl
from jax.experimental.pallas import tpu as pltpu
from jax.sharding import PartitionSpec as P

HEAD_DIM = 128
HEADS = 8
KV_HEADS = 2
BLOCK = 128
EXCHANGE_MAX_DEVICES = 16


EPSILON = 1e-06


def exclusive_prefix(state, axis, devices):
    total = jnp.zeros_like(state)
    window = state
    shift = 1
    while shift < devices:
        pairs = [(i, i + shift) for i in range(devices - shift)]
        got = lax.ppermute(window, axis, pairs)
        total = total + got
        if shift * 2 < devices:
            window = window + got
        shift *= 2
    return total


def attention_kernel(q_ref, *refs, per_group, kv_count):
    kv_refs = refs[:kv_count]
    code_ref = refs[kv_count]
    o_ref = refs[kv_count + 1]
    table = refs[kv_count + 2]
    offset = 0
    for ref in kv_refs:
        rows_in = ref.shape[0]
        table[offset:offset + rows_in, :] = ref[...]
        offset += rows_in
    keys_total = table.shape[0]
    keys = table[:, :HEAD_DIM]
    values = table[:, HEAD_DIM:]
    code = code_ref[...]
    rows = lax.broadcasted_iota(jnp.int32, (BLOCK, keys_total), 0)
    cols = lax.broadcasted_iota(jnp.int32, (BLOCK, keys_total), 1)
    cols = jnp.bitwise_and(cols, BLOCK - 1)
    allowed = (code == 1) | ((code == 2) & (cols <= rows))
    scale = HEAD_DIM ** (-0.5)
    for p in range(per_group):
        qp = q_ref[:, p * HEAD_DIM:(p + 1) * HEAD_DIM]
        scores = lax.dot_general(
            qp, keys, (((1,), (1,)), ((), ())), preferred_element_type=jnp.float32
        ) * scale
        scores = jnp.where(allowed, scores, -jnp.inf)
        highest = jnp.max(scores, axis=-1, keepdims=True)
        weights = jnp.where(allowed, jnp.exp(scores - highest), 0.0)
        total = jnp.sum(weights, axis=-1, keepdims=True)
        probs = (weights * (1.0 / total)).astype(jnp.bfloat16)
        out = jnp.dot(probs, values, preferred_element_type=jnp.float32)
        o_ref[:, p * HEAD_DIM:(p + 1) * HEAD_DIM] = out.astype(o_ref.dtype)


def kv_spec(piece):
    if piece.ndim == 3:
        return pl.BlockSpec((None, piece.shape[1], 2 * HEAD_DIM), lambda g, n: (g, 0, 0))
    return pl.BlockSpec((None, None, piece.shape[2], 2 * HEAD_DIM), lambda g, n: (g, n, 0, 0))


def attention(soft_query, pieces, code):
    tok_count = soft_query.shape[0]
    local_blocks = tok_count // BLOCK
    per_group = HEADS // KV_HEADS
    keys_total = code.shape[-1]
    width = per_group * HEAD_DIM
    flops = 4 * tok_count * HEADS * keys_total * HEAD_DIM
    bytes_accessed = 2 * (2 * soft_query.size + KV_HEADS * local_blocks * keys_total * 2 * HEAD_DIM)
    return pl.pallas_call(
        functools.partial(attention_kernel, per_group=per_group, kv_count=len(pieces)),
        out_shape=jax.ShapeDtypeStruct(soft_query.shape, jnp.bfloat16),
        grid=(KV_HEADS, local_blocks),
        in_specs=[pl.BlockSpec((BLOCK, width), lambda g, n: (n, g))]
        + [kv_spec(piece) for piece in pieces]
        + [pl.BlockSpec((None, None, 1, keys_total), lambda g, n: (g, n, 0, 0))],
        out_specs=pl.BlockSpec((BLOCK, width), lambda g, n: (n, g)),
        scratch_shapes=[pltpu.VMEM((keys_total, 2 * HEAD_DIM), jnp.bfloat16)],
        compiler_params=pltpu.CompilerParams(vmem_limit_bytes=48 * 1024 * 1024),
        cost_estimate=pl.CostEstimate(
            flops=flops, transcendentals=tok_count * HEADS * keys_total, bytes_accessed=bytes_accessed
        ),
    )(soft_query, *pieces, code)


def exchange_kv(packed, pattern, position, devices):
    tok_count = packed.shape[0]
    local_blocks = tok_count // BLOCK
    blocks = packed.reshape(local_blocks, BLOCK, KV_HEADS, 2 * HEAD_DIM)
    per_head = jnp.transpose(blocks, (2, 0, 1, 3)).reshape(KV_HEADS, tok_count, 2 * HEAD_DIM)
    pieces = [per_head]
    own_ids = position * local_blocks + jnp.arange(local_blocks, dtype=jnp.int32)
    ids = [jnp.broadcast_to(own_ids, (KV_HEADS, local_blocks))]
    if devices > 1:
        pairs = [(i, i + 1) for i in range(devices - 1)]
        pieces.append(lax.ppermute(per_head, "seq", pairs))
        near = own_ids - local_blocks
        ids.append(jnp.broadcast_to(jnp.where(position >= 1, near, -1), (KV_HEADS, local_blocks)))
    mine = lax.dynamic_slice_in_dim(pattern, position * local_blocks, local_blocks, 1)
    my_far = mine[:, :, 2:].reshape(KV_HEADS, -1)
    shifts = list(range(2, devices))
    if shifts:
        steps = jnp.array(shifts, jnp.int32)
        far_all = pattern[:, :, 2:].reshape(KV_HEADS, devices, -1)
        on_me = (far_all // local_blocks) == position
        choice_all = jnp.max(jnp.where(on_me, far_all - position * local_blocks, 0), axis=-1)
        dest_ids = jnp.arange(devices, dtype=jnp.int32)
        hit = dest_ids[None, :] == (position + steps)[:, None]
        choice = jnp.sum(jnp.where(hit[:, None, :], choice_all[None], 0), axis=-1)
        split = per_head.reshape(KV_HEADS, local_blocks, BLOCK, 2 * HEAD_DIM)
        chosen = split[None, :, 0]
        for j in range(1, local_blocks):
            chosen = jnp.where((choice == j)[:, :, None, None], split[None, :, j], chosen)
        sources = position - steps
        on_src = (my_far[None] // local_blocks) == sources[:, None, None]
        got = jnp.max(jnp.where(on_src, my_far[None], -1), axis=-1)
        got = jnp.where((sources >= 0)[:, None], got, -1)
    for i, shift in enumerate(shifts):
        pairs = [(k, k + shift) for k in range(devices - shift)]
        pieces.append(lax.ppermute(chosen[i], "seq", pairs))
        ids.append(got[i][:, None])
    slot_ids = jnp.concatenate(ids, axis=1)
    present = jnp.any(mine[:, :, :, None] == slot_ids[:, None, None, :], axis=2)
    present = present & (slot_ids >= 0)[:, None, :]
    own = mine[:, :, :1] == slot_ids[:, None, :]
    code = jnp.where(own, 2, present.astype(jnp.int32))
    return pieces, code


def local(
    hidden_in,
    lin_query,
    lin_key,
    lin_value,
    lin_gain,
    lin_out_weight,
    soft_gain,
    soft_wq,
    soft_wk,
    soft_wv,
    pattern,
    *,
    devices,
):
    tok_count = hidden_in.shape[0]
    local_blocks = tok_count // BLOCK
    per_group = HEADS // KV_HEADS
    listed = pattern.shape[2]
    position = lax.axis_index("seq")
    query_blocks = lin_query.reshape(local_blocks, BLOCK, KV_HEADS, per_group, HEAD_DIM)
    key_blocks = lin_key.reshape(local_blocks, BLOCK, KV_HEADS, HEAD_DIM)
    value_blocks = lin_value.reshape(local_blocks, BLOCK, KV_HEADS, HEAD_DIM)
    block_states = jnp.einsum(
        "ntgd,ntge->ngde", key_blocks, value_blocks, preferred_element_type=jnp.float32
    )
    device_state = jnp.sum(block_states, axis=0)
    carried = exclusive_prefix(device_state, "seq", devices)
    running = jnp.concatenate(
        [jnp.zeros_like(block_states[:1]), jnp.cumsum(block_states[:-1], axis=0)], axis=0
    )
    before = carried[None] + running
    inter = jnp.einsum(
        "ntgpd,ngde->ntgpe",
        query_blocks.astype(jnp.float32),
        before,
        precision=lax.Precision.HIGHEST,
    )
    rows_here = jnp.arange(BLOCK)
    causal = rows_here[:, None] >= rows_here[None, :]
    local_scores = jnp.einsum(
        "ntgpd,nsgd->ngpts", query_blocks, key_blocks, preferred_element_type=jnp.float32
    )
    local_scores = jnp.where(causal, local_scores, 0.0).astype(jnp.bfloat16)
    intra = jnp.einsum(
        "ngpts,nsge->ntgpe", local_scores, value_blocks, preferred_element_type=jnp.float32
    )
    mixed = (inter + intra).reshape(tok_count, HEADS, HEAD_DIM)
    normed = (
        mixed
        * lax.rsqrt(jnp.mean(mixed * mixed, axis=-1, keepdims=True) + EPSILON)
        * lin_gain.reshape(HEADS, HEAD_DIM)
    )
    normed = normed.reshape(tok_count, HEADS * HEAD_DIM).astype(jnp.bfloat16)
    branch = jnp.dot(normed, lin_out_weight, preferred_element_type=jnp.float32)
    residual = (hidden_in.astype(jnp.float32) + branch).astype(jnp.bfloat16)
    widened = residual.astype(jnp.float32)
    layer_in = (
        widened
        * lax.rsqrt(jnp.mean(widened * widened, axis=-1, keepdims=True) + EPSILON)
        * soft_gain
    ).astype(jnp.bfloat16)
    soft_key = jnp.dot(layer_in, soft_wk, preferred_element_type=jnp.float32).astype(jnp.bfloat16)
    soft_value = jnp.dot(layer_in, soft_wv, preferred_element_type=jnp.float32).astype(jnp.bfloat16)
    packed = jnp.concatenate(
        [
            soft_key.reshape(tok_count, KV_HEADS, HEAD_DIM),
            soft_value.reshape(tok_count, KV_HEADS, HEAD_DIM),
        ],
        axis=-1,
    )
    soft_query = jnp.dot(layer_in, soft_wq, preferred_element_type=jnp.float32).astype(jnp.bfloat16)

    if devices <= EXCHANGE_MAX_DEVICES:
        pieces, code = exchange_kv(packed, pattern, position, devices)
    else:
        whole = lax.all_gather(packed, "seq", axis=0, tiled=True)
        mine = lax.dynamic_slice_in_dim(pattern, position * local_blocks, local_blocks, 1)
        same = mine[..., :, None] == mine[..., None, :]
        earlier = jnp.arange(listed)[None, :] < jnp.arange(listed)[:, None]
        repeated = jnp.any(same & earlier, axis=-1)
        first_slot = (jnp.arange(listed) == 0)[None, None, :]
        code = jnp.where(first_slot, 2, jnp.logical_not(repeated).astype(jnp.int32))
        table = whole.reshape(-1, BLOCK, KV_HEADS, 2 * HEAD_DIM)
        group_ids = jnp.arange(KV_HEADS)[:, None, None]
        tiles = table[mine, :, group_ids, :]
        pieces = [tiles.reshape(KV_HEADS, local_blocks, listed * BLOCK, 2 * HEAD_DIM)]
    code = jnp.repeat(code, BLOCK, axis=-1)[:, :, None, :]
    return attention(soft_query, pieces, code)


def solution(mesh):
    in_specs = (
        P(("dp", "seq"), None),
        P(("dp", "seq"), None),
        P(("dp", "seq"), None),
        P(("dp", "seq"), None),
        P(),
        P(),
        P(),
        P(),
        P(),
        P(),
        P(),
    )
    out_specs = P(("dp", "seq"), None)
    body = functools.partial(local, devices=mesh.shape["seq"])
    return jax.shard_map(body, mesh=mesh, in_specs=in_specs, out_specs=out_specs, check_vma=False)
```

```python
import functools

import jax
import jax.numpy as jnp
from jax import lax
from jax.experimental import pallas as pl
from jax.experimental.pallas import tpu as pltpu
from jax.sharding import PartitionSpec as P

HEAD_DIM = 128
HEADS = 8
KV_HEADS = 2
BLOCK = 128
EXCHANGE_MAX_DEVICES = 16


EPSILON = 1e-06


def exclusive_prefix(state, axis, devices):
    total = jnp.zeros_like(state)
    window = state
    shift = 1
    while shift < devices:
        pairs = [(i, i + shift) for i in range(devices - shift)]
        got = lax.ppermute(window, axis, pairs)
        total = total + got
        if shift * 2 < devices:
            window = window + got
        shift *= 2
    return total


def attention_kernel(x_ref, w_ref, *refs, per_group, kv_count):
    q_all = jnp.dot(x_ref[...], w_ref[...], preferred_element_type=jnp.float32).astype(jnp.bfloat16)
    kv_refs = refs[:kv_count]
    code_ref = refs[kv_count]
    o_ref = refs[kv_count + 1]
    table = refs[kv_count + 2]
    offset = 0
    for ref in kv_refs:
        rows_in = ref.shape[0]
        table[offset:offset + rows_in, :] = ref[...]
        offset += rows_in
    keys_total = table.shape[0]
    keys = table[:, :HEAD_DIM]
    values = table[:, HEAD_DIM:]
    code = code_ref[...]
    rows = lax.broadcasted_iota(jnp.int32, (BLOCK, keys_total), 0)
    cols = lax.broadcasted_iota(jnp.int32, (BLOCK, keys_total), 1)
    cols = jnp.bitwise_and(cols, BLOCK - 1)
    allowed = (code == 1) | ((code == 2) & (cols <= rows))
    scale = HEAD_DIM ** (-0.5)
    for p in range(per_group):
        qp = q_all[:, p * HEAD_DIM:(p + 1) * HEAD_DIM]
        scores = lax.dot_general(
            qp, keys, (((1,), (1,)), ((), ())), preferred_element_type=jnp.float32
        ) * scale
        scores = jnp.where(allowed, scores, -jnp.inf)
        highest = jnp.max(scores, axis=-1, keepdims=True)
        weights = jnp.where(allowed, jnp.exp(scores - highest), 0.0)
        total = jnp.sum(weights, axis=-1, keepdims=True)
        probs = (weights * (1.0 / total)).astype(jnp.bfloat16)
        out = jnp.dot(probs, values, preferred_element_type=jnp.float32)
        o_ref[:, p * HEAD_DIM:(p + 1) * HEAD_DIM] = out.astype(o_ref.dtype)


def kv_spec(piece):
    if piece.ndim == 3:
        return pl.BlockSpec((None, piece.shape[1], 2 * HEAD_DIM), lambda g, n: (g, 0, 0))
    return pl.BlockSpec((None, None, piece.shape[2], 2 * HEAD_DIM), lambda g, n: (g, n, 0, 0))


def attention(layer_in, soft_wq, pieces, code):
    tok_count = layer_in.shape[0]
    local_blocks = tok_count // BLOCK
    per_group = HEADS // KV_HEADS
    keys_total = code.shape[-1]
    width = per_group * HEAD_DIM
    flops = 4 * tok_count * HEADS * keys_total * HEAD_DIM
    flops += 2 * tok_count * layer_in.shape[1] * soft_wq.shape[1]
    bytes_accessed = 2 * (layer_in.size + soft_wq.size + tok_count * soft_wq.shape[1])
    bytes_accessed += 2 * KV_HEADS * local_blocks * keys_total * 2 * HEAD_DIM
    return pl.pallas_call(
        functools.partial(attention_kernel, per_group=per_group, kv_count=len(pieces)),
        out_shape=jax.ShapeDtypeStruct((tok_count, soft_wq.shape[1]), jnp.bfloat16),
        grid=(KV_HEADS, local_blocks),
        in_specs=[
            pl.BlockSpec((BLOCK, layer_in.shape[1]), lambda g, n: (n, 0)),
            pl.BlockSpec((soft_wq.shape[0], width), lambda g, n: (0, g)),
        ]
        + [kv_spec(piece) for piece in pieces]
        + [pl.BlockSpec((None, None, 1, keys_total), lambda g, n: (g, n, 0, 0))],
        out_specs=pl.BlockSpec((BLOCK, width), lambda g, n: (n, g)),
        scratch_shapes=[pltpu.VMEM((keys_total, 2 * HEAD_DIM), jnp.bfloat16)],
        compiler_params=pltpu.CompilerParams(vmem_limit_bytes=48 * 1024 * 1024),
        cost_estimate=pl.CostEstimate(
            flops=flops, transcendentals=tok_count * HEADS * keys_total, bytes_accessed=bytes_accessed
        ),
    )(layer_in, soft_wq, *pieces, code)


def exchange_kv(packed, pattern, position, devices):
    tok_count = packed.shape[0]
    local_blocks = tok_count // BLOCK
    blocks = packed.reshape(local_blocks, BLOCK, KV_HEADS, 2 * HEAD_DIM)
    per_head = jnp.transpose(blocks, (2, 0, 1, 3)).reshape(KV_HEADS, tok_count, 2 * HEAD_DIM)
    pieces = [per_head]
    own_ids = position * local_blocks + jnp.arange(local_blocks, dtype=jnp.int32)
    ids = [jnp.broadcast_to(own_ids, (KV_HEADS, local_blocks))]
    if devices > 1:
        pairs = [(i, i + 1) for i in range(devices - 1)]
        pieces.append(lax.ppermute(per_head, "seq", pairs))
        near = own_ids - local_blocks
        ids.append(jnp.broadcast_to(jnp.where(position >= 1, near, -1), (KV_HEADS, local_blocks)))
    mine = lax.dynamic_slice_in_dim(pattern, position * local_blocks, local_blocks, 1)
    my_far = mine[:, :, 2:].reshape(KV_HEADS, -1)
    shifts = list(range(2, devices))
    if shifts:
        steps = jnp.array(shifts, jnp.int32)
        far_all = pattern[:, :, 2:].reshape(KV_HEADS, devices, -1)
        on_me = (far_all // local_blocks) == position
        choice_all = jnp.max(jnp.where(on_me, far_all - position * local_blocks, 0), axis=-1)
        dest_ids = jnp.arange(devices, dtype=jnp.int32)
        hit = dest_ids[None, :] == (position + steps)[:, None]
        choice = jnp.sum(jnp.where(hit[:, None, :], choice_all[None], 0), axis=-1)
        split = per_head.reshape(KV_HEADS, local_blocks, BLOCK, 2 * HEAD_DIM)
        chosen = split[None, :, 0]
        for j in range(1, local_blocks):
            chosen = jnp.where((choice == j)[:, :, None, None], split[None, :, j], chosen)
        sources = position - steps
        on_src = (my_far[None] // local_blocks) == sources[:, None, None]
        got = jnp.max(jnp.where(on_src, my_far[None], -1), axis=-1)
        got = jnp.where((sources >= 0)[:, None], got, -1)
    for i, shift in enumerate(shifts):
        pairs = [(k, k + shift) for k in range(devices - shift)]
        pieces.append(lax.ppermute(chosen[i], "seq", pairs))
        ids.append(got[i][:, None])
    slot_ids = jnp.concatenate(ids, axis=1)
    present = jnp.any(mine[:, :, :, None] == slot_ids[:, None, None, :], axis=2)
    present = present & (slot_ids >= 0)[:, None, :]
    own = mine[:, :, :1] == slot_ids[:, None, :]
    code = jnp.where(own, 2, present.astype(jnp.int32))
    return pieces, code


def local(
    hidden_in,
    lin_query,
    lin_key,
    lin_value,
    lin_gain,
    lin_out_weight,
    soft_gain,
    soft_wq,
    soft_wk,
    soft_wv,
    pattern,
    *,
    devices,
):
    tok_count = hidden_in.shape[0]
    local_blocks = tok_count // BLOCK
    per_group = HEADS // KV_HEADS
    listed = pattern.shape[2]
    position = lax.axis_index("seq")
    query_blocks = lin_query.reshape(local_blocks, BLOCK, KV_HEADS, per_group, HEAD_DIM)
    key_blocks = lin_key.reshape(local_blocks, BLOCK, KV_HEADS, HEAD_DIM)
    value_blocks = lin_value.reshape(local_blocks, BLOCK, KV_HEADS, HEAD_DIM)
    block_states = jnp.einsum(
        "ntgd,ntge->ngde", key_blocks, value_blocks, preferred_element_type=jnp.float32
    )
    device_state = jnp.sum(block_states, axis=0)
    carried = exclusive_prefix(device_state, "seq", devices)
    running = jnp.concatenate(
        [jnp.zeros_like(block_states[:1]), jnp.cumsum(block_states[:-1], axis=0)], axis=0
    )
    before = carried[None] + running
    inter = jnp.einsum(
        "ntgpd,ngde->ntgpe",
        query_blocks.astype(jnp.float32),
        before,
        precision=lax.Precision.HIGHEST,
    )
    rows_here = jnp.arange(BLOCK)
    causal = rows_here[:, None] >= rows_here[None, :]
    local_scores = jnp.einsum(
        "ntgpd,nsgd->ngpts", query_blocks, key_blocks, preferred_element_type=jnp.float32
    )
    local_scores = jnp.where(causal, local_scores, 0.0).astype(jnp.bfloat16)
    intra = jnp.einsum(
        "ngpts,nsge->ntgpe", local_scores, value_blocks, preferred_element_type=jnp.float32
    )
    mixed = (inter + intra).reshape(tok_count, HEADS, HEAD_DIM)
    normed = (
        mixed
        * lax.rsqrt(jnp.mean(mixed * mixed, axis=-1, keepdims=True) + EPSILON)
        * lin_gain.reshape(HEADS, HEAD_DIM)
    )
    normed = normed.reshape(tok_count, HEADS * HEAD_DIM).astype(jnp.bfloat16)
    branch = jnp.dot(normed, lin_out_weight, preferred_element_type=jnp.float32)
    residual = (hidden_in.astype(jnp.float32) + branch).astype(jnp.bfloat16)
    widened = residual.astype(jnp.float32)
    layer_in = (
        widened
        * lax.rsqrt(jnp.mean(widened * widened, axis=-1, keepdims=True) + EPSILON)
        * soft_gain
    ).astype(jnp.bfloat16)
    soft_key = jnp.dot(layer_in, soft_wk, preferred_element_type=jnp.float32).astype(jnp.bfloat16)
    soft_value = jnp.dot(layer_in, soft_wv, preferred_element_type=jnp.float32).astype(jnp.bfloat16)
    packed = jnp.concatenate(
        [
            soft_key.reshape(tok_count, KV_HEADS, HEAD_DIM),
            soft_value.reshape(tok_count, KV_HEADS, HEAD_DIM),
        ],
        axis=-1,
    )

    if devices <= EXCHANGE_MAX_DEVICES:
        pieces, code = exchange_kv(packed, pattern, position, devices)
    else:
        whole = lax.all_gather(packed, "seq", axis=0, tiled=True)
        mine = lax.dynamic_slice_in_dim(pattern, position * local_blocks, local_blocks, 1)
        same = mine[..., :, None] == mine[..., None, :]
        earlier = jnp.arange(listed)[None, :] < jnp.arange(listed)[:, None]
        repeated = jnp.any(same & earlier, axis=-1)
        first_slot = (jnp.arange(listed) == 0)[None, None, :]
        code = jnp.where(first_slot, 2, jnp.logical_not(repeated).astype(jnp.int32))
        table = whole.reshape(-1, BLOCK, KV_HEADS, 2 * HEAD_DIM)
        group_ids = jnp.arange(KV_HEADS)[:, None, None]
        tiles = table[mine, :, group_ids, :]
        pieces = [tiles.reshape(KV_HEADS, local_blocks, listed * BLOCK, 2 * HEAD_DIM)]
    code = jnp.repeat(code, BLOCK, axis=-1)[:, :, None, :]
    return attention(layer_in, soft_wq, pieces, code)


def solution(mesh):
    in_specs = (
        P(("dp", "seq"), None),
        P(("dp", "seq"), None),
        P(("dp", "seq"), None),
        P(("dp", "seq"), None),
        P(),
        P(),
        P(),
        P(),
        P(),
        P(),
        P(),
    )
    out_specs = P(("dp", "seq"), None)
    body = functools.partial(local, devices=mesh.shape["seq"])
    return jax.shard_map(body, mesh=mesh, in_specs=in_specs, out_specs=out_specs, check_vma=False)
```

```python
import functools

import jax
import jax.numpy as jnp
from jax import lax
from jax.experimental import pallas as pl
from jax.experimental.pallas import tpu as pltpu
from jax.sharding import PartitionSpec as P


HEAD_DIM = 128
HEADS = 8
KV_HEADS = 2
BLOCK = 128
EXCHANGE_MAX_DEVICES = 16


EPSILON = 1e-06


def exclusive_prefix(state, axis, devices):
    total = jnp.zeros_like(state)
    window = state
    shift = 1
    while shift < devices:
        pairs = [(i, i + shift) for i in range(devices - shift)]
        got = lax.ppermute(window, axis, pairs)
        total = total + got
        if shift * 2 < devices:
            window = window + got
        shift *= 2
    return total


def slot_ids_exchange(pat_ref, pos, g, nblk, listed, devices, local_blocks):
    ids = [pos * local_blocks + c for c in range(local_blocks)]
    ids += [jnp.where(pos >= 1, (pos - 1) * local_blocks + c, -1) for c in range(local_blocks)]
    for shift in range(2, devices):
        src = pos - shift
        low = src * local_blocks
        best = jnp.int32(-1)
        for j in range(local_blocks):
            row = (g * nblk + pos * local_blocks + j) * listed
            for k in range(2, listed):
                entry = pat_ref[row + k]
                inside = (entry >= low) & (entry < low + local_blocks)
                best = jnp.where(inside & (entry > best), entry, best)
        ids.append(jnp.where(src >= 0, best, -1))
    return ids


def attention_kernel(pat_ref, pos_ref, q_ref, *refs, per_group, kv_count, devices, exchange, nblk, listed):
    kv_refs = refs[:kv_count]
    o_ref = refs[kv_count]
    table = refs[kv_count + 1]
    g = pl.program_id(0)
    n = pl.program_id(1)
    pos = pos_ref[0]
    offset = 0
    for ref in kv_refs:
        rows_in = ref.shape[0]
        table[offset:offset + rows_in, :] = ref[...]
        offset += rows_in
    keys_total = table.shape[0]
    slots = keys_total // BLOCK
    lb = nblk // devices
    row = (g * nblk + pos * lb + n) * listed
    first = pat_ref[row]
    if exchange:
        ids = slot_ids_exchange(pat_ref, pos, g, nblk, listed, devices, lb)
        codes = []
        for bid in ids:
            hit = jnp.int32(0)
            for j in range(listed):
                hit = jnp.where(pat_ref[row + j] == bid, 1, hit)
            hit = jnp.where(bid >= 0, hit, 0)
            codes.append(jnp.where(bid == first, 2, hit))
    else:
        codes = [jnp.int32(2)]
        for c in range(1, slots):
            entry = pat_ref[row + c]
            seen = jnp.int32(0)
            for j in range(c):
                seen = jnp.where(pat_ref[row + j] == entry, 1, seen)
            codes.append(1 - seen)
    slot_of_col = lax.broadcasted_iota(jnp.int32, (1, keys_total), 1) // BLOCK
    code = jnp.zeros((1, keys_total), jnp.int32)
    for c in range(slots):
        code = jnp.where(slot_of_col == c, codes[c], code)
    keys = table[:, :HEAD_DIM]
    values = table[:, HEAD_DIM:]
    rows = lax.broadcasted_iota(jnp.int32, (BLOCK, keys_total), 0)
    cols = lax.broadcasted_iota(jnp.int32, (BLOCK, keys_total), 1)
    cols = jnp.bitwise_and(cols, BLOCK - 1)
    allowed = (code == 1) | ((code == 2) & (cols <= rows))
    scale = HEAD_DIM ** (-0.5)
    for p in range(per_group):
        qp = q_ref[:, p * HEAD_DIM:(p + 1) * HEAD_DIM]
        scores = lax.dot_general(
            qp, keys, (((1,), (1,)), ((), ())), preferred_element_type=jnp.float32
        ) * scale
        scores = jnp.where(allowed, scores, -jnp.inf)
        highest = jnp.max(scores, axis=-1, keepdims=True)
        weights = jnp.where(allowed, jnp.exp(scores - highest), 0.0)
        total = jnp.sum(weights, axis=-1, keepdims=True)
        probs = (weights * (1.0 / total)).astype(jnp.bfloat16)
        out = jnp.dot(probs, values, preferred_element_type=jnp.float32)
        o_ref[:, p * HEAD_DIM:(p + 1) * HEAD_DIM] = out.astype(o_ref.dtype)


def kv_spec(piece):
    if piece.ndim == 3:
        return pl.BlockSpec((None, piece.shape[1], 2 * HEAD_DIM), lambda g, n, pat, pos: (g, 0, 0))
    return pl.BlockSpec((None, None, piece.shape[2], 2 * HEAD_DIM), lambda g, n, pat, pos: (g, n, 0, 0))


def attention(soft_query, pieces, pattern, position, devices, exchange):
    tok_count = soft_query.shape[0]
    local_blocks = tok_count // BLOCK
    per_group = HEADS // KV_HEADS
    keys_total = sum(piece.shape[-2] for piece in pieces)
    width = per_group * HEAD_DIM
    flops = 4 * tok_count * HEADS * keys_total * HEAD_DIM
    bytes_accessed = 2 * (2 * soft_query.size + KV_HEADS * local_blocks * keys_total * 2 * HEAD_DIM)
    kernel = functools.partial(
        attention_kernel,
        per_group=per_group,
        kv_count=len(pieces),
        devices=devices,
        exchange=exchange,
        nblk=pattern.shape[1],
        listed=pattern.shape[2],
    )
    grid_spec = pltpu.PrefetchScalarGridSpec(
        num_scalar_prefetch=2,
        grid=(KV_HEADS, local_blocks),
        in_specs=[pl.BlockSpec((BLOCK, width), lambda g, n, pat, pos: (n, g))]
        + [kv_spec(piece) for piece in pieces],
        out_specs=pl.BlockSpec((BLOCK, width), lambda g, n, pat, pos: (n, g)),
        scratch_shapes=[pltpu.VMEM((keys_total, 2 * HEAD_DIM), jnp.bfloat16)],
    )
    return pl.pallas_call(
        kernel,
        out_shape=jax.ShapeDtypeStruct(soft_query.shape, jnp.bfloat16),
        grid_spec=grid_spec,
        compiler_params=pltpu.CompilerParams(vmem_limit_bytes=48 * 1024 * 1024),
        cost_estimate=pl.CostEstimate(
            flops=flops, transcendentals=tok_count * HEADS * keys_total, bytes_accessed=bytes_accessed
        ),
    )(pattern.reshape(-1), position.reshape(1).astype(jnp.int32), soft_query, *pieces)


def exchange_kv(packed, pattern, position, devices):
    tok_count = packed.shape[0]
    local_blocks = tok_count // BLOCK
    blocks = packed.reshape(local_blocks, BLOCK, KV_HEADS, 2 * HEAD_DIM)
    per_head = jnp.transpose(blocks, (2, 0, 1, 3)).reshape(KV_HEADS, tok_count, 2 * HEAD_DIM)
    pieces = [per_head]
    if devices > 1:
        pairs = [(i, i + 1) for i in range(devices - 1)]
        pieces.append(lax.ppermute(per_head, "seq", pairs))
    shifts = list(range(2, devices))
    if shifts:
        steps = jnp.array(shifts, jnp.int32)
        far_all = pattern[:, :, 2:].reshape(KV_HEADS, devices, -1)
        on_me = (far_all // local_blocks) == position
        choice_all = jnp.max(jnp.where(on_me, far_all - position * local_blocks, 0), axis=-1)
        dest_ids = jnp.arange(devices, dtype=jnp.int32)
        hit = dest_ids[None, :] == (position + steps)[:, None]
        choice = jnp.sum(jnp.where(hit[:, None, :], choice_all[None], 0), axis=-1)
        split = per_head.reshape(KV_HEADS, local_blocks, BLOCK, 2 * HEAD_DIM)
        chosen = split[None, :, 0]
        for j in range(1, local_blocks):
            chosen = jnp.where((choice == j)[:, :, None, None], split[None, :, j], chosen)
    for i, shift in enumerate(shifts):
        pairs = [(k, k + shift) for k in range(devices - shift)]
        pieces.append(lax.ppermute(chosen[i], "seq", pairs))
    return pieces


def local(
    hidden_in,
    lin_query,
    lin_key,
    lin_value,
    lin_gain,
    lin_out_weight,
    soft_gain,
    soft_wq,
    soft_wk,
    soft_wv,
    pattern,
    *,
    devices,
):
    tok_count = hidden_in.shape[0]
    local_blocks = tok_count // BLOCK
    per_group = HEADS // KV_HEADS
    listed = pattern.shape[2]
    position = lax.axis_index("seq")
    query_blocks = lin_query.reshape(local_blocks, BLOCK, KV_HEADS, per_group, HEAD_DIM)
    key_blocks = lin_key.reshape(local_blocks, BLOCK, KV_HEADS, HEAD_DIM)
    value_blocks = lin_value.reshape(local_blocks, BLOCK, KV_HEADS, HEAD_DIM)
    block_states = jnp.einsum(
        "ntgd,ntge->ngde", key_blocks, value_blocks, preferred_element_type=jnp.float32
    )
    device_state = jnp.sum(block_states, axis=0)
    carried = exclusive_prefix(device_state, "seq", devices)
    running = jnp.concatenate(
        [jnp.zeros_like(block_states[:1]), jnp.cumsum(block_states[:-1], axis=0)], axis=0
    )
    before = carried[None] + running
    inter = jnp.einsum(
        "ntgpd,ngde->ntgpe",
        query_blocks.astype(jnp.float32),
        before,
        precision=lax.Precision.HIGHEST,
    )
    rows_here = jnp.arange(BLOCK)
    causal = rows_here[:, None] >= rows_here[None, :]
    local_scores = jnp.einsum(
        "ntgpd,nsgd->ngpts", query_blocks, key_blocks, preferred_element_type=jnp.float32
    )
    local_scores = jnp.where(causal, local_scores, 0.0).astype(jnp.bfloat16)
    intra = jnp.einsum(
        "ngpts,nsge->ntgpe", local_scores, value_blocks, preferred_element_type=jnp.float32
    )
    mixed = (inter + intra).reshape(tok_count, HEADS, HEAD_DIM)
    normed = (
        mixed
        * lax.rsqrt(jnp.mean(mixed * mixed, axis=-1, keepdims=True) + EPSILON)
        * lin_gain.reshape(HEADS, HEAD_DIM)
    )
    normed = normed.reshape(tok_count, HEADS * HEAD_DIM).astype(jnp.bfloat16)
    branch = jnp.dot(normed, lin_out_weight, preferred_element_type=jnp.float32)
    residual = (hidden_in.astype(jnp.float32) + branch).astype(jnp.bfloat16)
    widened = residual.astype(jnp.float32)
    layer_in = (
        widened
        * lax.rsqrt(jnp.mean(widened * widened, axis=-1, keepdims=True) + EPSILON)
        * soft_gain
    ).astype(jnp.bfloat16)
    soft_key = jnp.dot(layer_in, soft_wk, preferred_element_type=jnp.float32).astype(jnp.bfloat16)
    soft_value = jnp.dot(layer_in, soft_wv, preferred_element_type=jnp.float32).astype(jnp.bfloat16)
    packed = jnp.concatenate(
        [
            soft_key.reshape(tok_count, KV_HEADS, HEAD_DIM),
            soft_value.reshape(tok_count, KV_HEADS, HEAD_DIM),
        ],
        axis=-1,
    )
    soft_query = jnp.dot(layer_in, soft_wq, preferred_element_type=jnp.float32).astype(jnp.bfloat16)

    exchange = devices <= EXCHANGE_MAX_DEVICES
    if exchange:
        pieces = exchange_kv(packed, pattern, position, devices)
    else:
        whole = lax.all_gather(packed, "seq", axis=0, tiled=True)
        mine = lax.dynamic_slice_in_dim(pattern, position * local_blocks, local_blocks, 1)
        table = whole.reshape(-1, BLOCK, KV_HEADS, 2 * HEAD_DIM)
        group_ids = jnp.arange(KV_HEADS)[:, None, None]
        tiles = table[mine, :, group_ids, :]
        pieces = [tiles.reshape(KV_HEADS, local_blocks, listed * BLOCK, 2 * HEAD_DIM)]
    return attention(soft_query, pieces, pattern, position, devices, exchange)


def solution(mesh):
    in_specs = (
        P(("dp", "seq"), None),
        P(("dp", "seq"), None),
        P(("dp", "seq"), None),
        P(("dp", "seq"), None),
        P(),
        P(),
        P(),
        P(),
        P(),
        P(),
        P(),
    )
    out_specs = P(("dp", "seq"), None)
    devices = mesh.shape["seq"]
    body = functools.partial(local, devices=devices)
    return jax.shard_map(body, mesh=mesh, in_specs=in_specs, out_specs=out_specs, check_vma=False)
```

```python
import functools

import jax
import jax.numpy as jnp
from jax import lax
from jax.experimental import pallas as pl
from jax.experimental.pallas import tpu as pltpu
from jax.sharding import PartitionSpec as P


HEAD_DIM = 128
HEADS = 8
KV_HEADS = 2
BLOCK = 128
EXCHANGE_MAX_DEVICES = 16


EPSILON = 1e-06


def exclusive_prefix(state, axis, devices):
    total = jnp.zeros_like(state)
    window = state
    shift = 1
    while shift < devices:
        pairs = [(i, i + shift) for i in range(devices - shift)]
        got = lax.ppermute(window, axis, pairs)
        total = total + got
        if shift * 2 < devices:
            window = window + got
        shift *= 2
    return total


def slot_ids_exchange(pat_ref, pos, g, nblk, listed, devices, local_blocks):
    ids = [pos * local_blocks + c for c in range(local_blocks)]
    ids += [jnp.where(pos >= 1, (pos - 1) * local_blocks + c, -1) for c in range(local_blocks)]
    for shift in range(2, devices):
        src = pos - shift
        low = src * local_blocks
        best = jnp.int32(-1)
        for j in range(local_blocks):
            row = (g * nblk + pos * local_blocks + j) * listed
            for k in range(2, listed):
                entry = pat_ref[row + k]
                inside = (entry >= low) & (entry < low + local_blocks)
                best = jnp.where(inside & (entry > best), entry, best)
        ids.append(jnp.where(src >= 0, best, -1))
    return ids


def attention_kernel(pat_ref, pos_ref, q_ref, *refs, per_group, kv_count, devices, exchange, nblk, listed):
    kv_refs = refs[:kv_count]
    o_ref = refs[kv_count]
    table = refs[kv_count + 1]
    g = pl.program_id(0)
    n = pl.program_id(1)
    pos = pos_ref[0]
    offset = 0
    for ref in kv_refs:
        rows_in = ref.shape[0]
        table[offset:offset + rows_in, :] = ref[...]
        offset += rows_in
    keys_total = table.shape[0]
    slots = keys_total // BLOCK
    lb = nblk // devices
    row = (g * nblk + pos * lb + n) * listed
    first = pat_ref[row]
    if exchange:
        ids = slot_ids_exchange(pat_ref, pos, g, nblk, listed, devices, lb)
        codes = []
        for bid in ids:
            hit = jnp.int32(0)
            for j in range(listed):
                hit = jnp.where(pat_ref[row + j] == bid, 1, hit)
            hit = jnp.where(bid >= 0, hit, 0)
            codes.append(jnp.where(bid == first, 2, hit))
    else:
        codes = [jnp.int32(2)]
        for c in range(1, slots):
            entry = pat_ref[row + c]
            seen = jnp.int32(0)
            for j in range(c):
                seen = jnp.where(pat_ref[row + j] == entry, 1, seen)
            codes.append(1 - seen)
    slot_of_col = lax.broadcasted_iota(jnp.int32, (1, keys_total), 1) // BLOCK
    code = jnp.zeros((1, keys_total), jnp.int32)
    for c in range(slots):
        code = jnp.where(slot_of_col == c, codes[c], code)
    keys = table[:, :HEAD_DIM]
    values = table[:, HEAD_DIM:]
    rows = lax.broadcasted_iota(jnp.int32, (BLOCK, keys_total), 0)
    cols = lax.broadcasted_iota(jnp.int32, (BLOCK, keys_total), 1)
    cols = jnp.bitwise_and(cols, BLOCK - 1)
    allowed = (code == 1) | ((code == 2) & (cols <= rows))
    scale = HEAD_DIM ** (-0.5)
    for p in range(per_group):
        qp = q_ref[:, p * HEAD_DIM:(p + 1) * HEAD_DIM]
        scores = lax.dot_general(
            qp, keys, (((1,), (1,)), ((), ())), preferred_element_type=jnp.float32
        ) * scale
        scores = jnp.where(allowed, scores, -jnp.inf)
        highest = jnp.max(scores, axis=-1, keepdims=True)
        weights = jnp.where(allowed, jnp.exp(scores - highest), 0.0)
        total = jnp.sum(weights, axis=-1, keepdims=True)
        probs = (weights * (1.0 / total)).astype(jnp.bfloat16)
        out = jnp.dot(probs, values, preferred_element_type=jnp.float32)
        o_ref[:, p * HEAD_DIM:(p + 1) * HEAD_DIM] = out.astype(o_ref.dtype)


def kv_spec(piece):
    if piece.ndim == 3:
        return pl.BlockSpec((None, piece.shape[1], 2 * HEAD_DIM), lambda g, n, pat, pos: (g, 0, 0))
    return pl.BlockSpec((None, None, piece.shape[2], 2 * HEAD_DIM), lambda g, n, pat, pos: (g, n, 0, 0))


def attention(soft_query, pieces, pattern, position, devices, exchange):
    tok_count = soft_query.shape[0]
    local_blocks = tok_count // BLOCK
    per_group = HEADS // KV_HEADS
    keys_total = sum(piece.shape[-2] for piece in pieces)
    width = per_group * HEAD_DIM
    flops = 4 * tok_count * HEADS * keys_total * HEAD_DIM
    bytes_accessed = 2 * (2 * soft_query.size + KV_HEADS * local_blocks * keys_total * 2 * HEAD_DIM)
    kernel = functools.partial(
        attention_kernel,
        per_group=per_group,
        kv_count=len(pieces),
        devices=devices,
        exchange=exchange,
        nblk=pattern.shape[1],
        listed=pattern.shape[2],
    )
    grid_spec = pltpu.PrefetchScalarGridSpec(
        num_scalar_prefetch=2,
        grid=(KV_HEADS, local_blocks),
        in_specs=[pl.BlockSpec((BLOCK, width), lambda g, n, pat, pos: (n, g))]
        + [kv_spec(piece) for piece in pieces],
        out_specs=pl.BlockSpec((BLOCK, width), lambda g, n, pat, pos: (n, g)),
        scratch_shapes=[pltpu.VMEM((keys_total, 2 * HEAD_DIM), jnp.bfloat16)],
    )
    return pl.pallas_call(
        kernel,
        out_shape=jax.ShapeDtypeStruct(soft_query.shape, jnp.bfloat16),
        grid_spec=grid_spec,
        compiler_params=pltpu.CompilerParams(vmem_limit_bytes=48 * 1024 * 1024),
        cost_estimate=pl.CostEstimate(
            flops=flops, transcendentals=tok_count * HEADS * keys_total, bytes_accessed=bytes_accessed
        ),
    )(pattern.reshape(-1), position.reshape(1).astype(jnp.int32), soft_query, *pieces)


def post_mix_kernel(
    mixed_ref, lin_gain_ref, lin_out_ref, hidden_ref, soft_gain_ref, wk_ref, wv_ref, wq_ref,
    kv_ref, q_ref, normed_ref,
):
    for h in range(HEADS):
        part = mixed_ref[:, h * HEAD_DIM:(h + 1) * HEAD_DIM]
        power = jnp.mean(part * part, axis=-1, keepdims=True)
        gain = lin_gain_ref[:, h * HEAD_DIM:(h + 1) * HEAD_DIM]
        normed_ref[:, h * HEAD_DIM:(h + 1) * HEAD_DIM] = (
            part * lax.rsqrt(power + EPSILON) * gain
        ).astype(jnp.bfloat16)
    branch = jnp.dot(normed_ref[...], lin_out_ref[...], preferred_element_type=jnp.float32)
    residual = (hidden_ref[...].astype(jnp.float32) + branch).astype(jnp.bfloat16)
    widened = residual.astype(jnp.float32)
    power = jnp.mean(widened * widened, axis=-1, keepdims=True)
    layer_in = (widened * lax.rsqrt(power + EPSILON) * soft_gain_ref[...]).astype(jnp.bfloat16)
    keys = jnp.dot(layer_in, wk_ref[...], preferred_element_type=jnp.float32).astype(jnp.bfloat16)
    values = jnp.dot(layer_in, wv_ref[...], preferred_element_type=jnp.float32).astype(jnp.bfloat16)
    for g in range(KV_HEADS):
        kv_ref[g, :, :HEAD_DIM] = keys[:, g * HEAD_DIM:(g + 1) * HEAD_DIM]
        kv_ref[g, :, HEAD_DIM:] = values[:, g * HEAD_DIM:(g + 1) * HEAD_DIM]
    q_ref[...] = jnp.dot(layer_in, wq_ref[...], preferred_element_type=jnp.float32).astype(jnp.bfloat16)


def post_mix(mixed, lin_gain, lin_out_weight, hidden_in, soft_gain, soft_wk, soft_wv, soft_wq):
    tok_count, width = mixed.shape
    model = hidden_in.shape[1]
    steps = tok_count // BLOCK
    whole = lambda i: (0, 0)
    flops = 2 * tok_count * (width * model + model * (soft_wk.shape[1] + soft_wv.shape[1] + soft_wq.shape[1]))
    bytes_accessed = 4 * mixed.size + 2 * (lin_out_weight.size + hidden_in.size + soft_wk.size + soft_wv.size + soft_wq.size)
    return pl.pallas_call(
        post_mix_kernel,
        out_shape=(
            jax.ShapeDtypeStruct((KV_HEADS, tok_count, 2 * HEAD_DIM), jnp.bfloat16),
            jax.ShapeDtypeStruct((tok_count, soft_wq.shape[1]), jnp.bfloat16),
        ),
        grid=(steps,),
        in_specs=[
            pl.BlockSpec((BLOCK, width), lambda i: (i, 0)),
            pl.BlockSpec((1, width), whole),
            pl.BlockSpec(lin_out_weight.shape, whole),
            pl.BlockSpec((BLOCK, model), lambda i: (i, 0)),
            pl.BlockSpec((1, model), whole),
            pl.BlockSpec(soft_wk.shape, whole),
            pl.BlockSpec(soft_wv.shape, whole),
            pl.BlockSpec(soft_wq.shape, whole),
        ],
        out_specs=(
            pl.BlockSpec((KV_HEADS, BLOCK, 2 * HEAD_DIM), lambda i: (0, i, 0)),
            pl.BlockSpec((BLOCK, soft_wq.shape[1]), lambda i: (i, 0)),
        ),
        scratch_shapes=[pltpu.VMEM((BLOCK, width), jnp.bfloat16)],
        compiler_params=pltpu.CompilerParams(vmem_limit_bytes=56 * 1024 * 1024),
        cost_estimate=pl.CostEstimate(flops=flops, transcendentals=0, bytes_accessed=bytes_accessed),
    )(
        mixed,
        lin_gain.reshape(1, -1),
        lin_out_weight,
        hidden_in,
        soft_gain.reshape(1, -1),
        soft_wk,
        soft_wv,
        soft_wq,
    )


def exchange_kv(per_head, pattern, position, devices):
    tok_count = per_head.shape[1]
    local_blocks = tok_count // BLOCK
    pieces = [per_head]
    if devices > 1:
        pairs = [(i, i + 1) for i in range(devices - 1)]
        pieces.append(lax.ppermute(per_head, "seq", pairs))
    shifts = list(range(2, devices))
    if shifts:
        steps = jnp.array(shifts, jnp.int32)
        far_all = pattern[:, :, 2:].reshape(KV_HEADS, devices, -1)
        on_me = (far_all // local_blocks) == position
        choice_all = jnp.max(jnp.where(on_me, far_all - position * local_blocks, 0), axis=-1)
        dest_ids = jnp.arange(devices, dtype=jnp.int32)
        hit = dest_ids[None, :] == (position + steps)[:, None]
        choice = jnp.sum(jnp.where(hit[:, None, :], choice_all[None], 0), axis=-1)
        split = per_head.reshape(KV_HEADS, local_blocks, BLOCK, 2 * HEAD_DIM)
        chosen = split[None, :, 0]
        for j in range(1, local_blocks):
            chosen = jnp.where((choice == j)[:, :, None, None], split[None, :, j], chosen)
    for i, shift in enumerate(shifts):
        pairs = [(k, k + shift) for k in range(devices - shift)]
        pieces.append(lax.ppermute(chosen[i], "seq", pairs))
    return pieces


def local(
    hidden_in,
    lin_query,
    lin_key,
    lin_value,
    lin_gain,
    lin_out_weight,
    soft_gain,
    soft_wq,
    soft_wk,
    soft_wv,
    pattern,
    *,
    devices,
):
    tok_count = hidden_in.shape[0]
    local_blocks = tok_count // BLOCK
    per_group = HEADS // KV_HEADS
    listed = pattern.shape[2]
    position = lax.axis_index("seq")
    query_blocks = lin_query.reshape(local_blocks, BLOCK, KV_HEADS, per_group, HEAD_DIM)
    key_blocks = lin_key.reshape(local_blocks, BLOCK, KV_HEADS, HEAD_DIM)
    value_blocks = lin_value.reshape(local_blocks, BLOCK, KV_HEADS, HEAD_DIM)
    block_states = jnp.einsum(
        "ntgd,ntge->ngde", key_blocks, value_blocks, preferred_element_type=jnp.float32
    )
    device_state = jnp.sum(block_states, axis=0)
    carried = exclusive_prefix(device_state, "seq", devices)
    running = jnp.concatenate(
        [jnp.zeros_like(block_states[:1]), jnp.cumsum(block_states[:-1], axis=0)], axis=0
    )
    before = carried[None] + running
    inter = jnp.einsum(
        "ntgpd,ngde->ntgpe",
        query_blocks.astype(jnp.float32),
        before,
        precision=lax.Precision.HIGHEST,
    )
    rows_here = jnp.arange(BLOCK)
    causal = rows_here[:, None] >= rows_here[None, :]
    local_scores = jnp.einsum(
        "ntgpd,nsgd->ngpts", query_blocks, key_blocks, preferred_element_type=jnp.float32
    )
    local_scores = jnp.where(causal, local_scores, 0.0).astype(jnp.bfloat16)
    intra = jnp.einsum(
        "ngpts,nsge->ntgpe", local_scores, value_blocks, preferred_element_type=jnp.float32
    )
    mixed = (inter + intra).reshape(tok_count, HEADS * HEAD_DIM)
    per_head, soft_query = post_mix(
        mixed, lin_gain, lin_out_weight, hidden_in, soft_gain, soft_wk, soft_wv, soft_wq
    )

    exchange = devices <= EXCHANGE_MAX_DEVICES
    if exchange:
        pieces = exchange_kv(per_head, pattern, position, devices)
    else:
        packed = jnp.transpose(per_head, (1, 0, 2))
        whole = lax.all_gather(packed, "seq", axis=0, tiled=True)
        mine = lax.dynamic_slice_in_dim(pattern, position * local_blocks, local_blocks, 1)
        table = whole.reshape(-1, BLOCK, KV_HEADS, 2 * HEAD_DIM)
        group_ids = jnp.arange(KV_HEADS)[:, None, None]
        tiles = table[mine, :, group_ids, :]
        pieces = [tiles.reshape(KV_HEADS, local_blocks, listed * BLOCK, 2 * HEAD_DIM)]
    return attention(soft_query, pieces, pattern, position, devices, exchange)


def solution(mesh):
    in_specs = (
        P(("dp", "seq"), None),
        P(("dp", "seq"), None),
        P(("dp", "seq"), None),
        P(("dp", "seq"), None),
        P(),
        P(),
        P(),
        P(),
        P(),
        P(),
        P(),
    )
    out_specs = P(("dp", "seq"), None)
    devices = mesh.shape["seq"]
    body = functools.partial(local, devices=devices)
    return jax.shard_map(body, mesh=mesh, in_specs=in_specs, out_specs=out_specs, check_vma=False)
```

```python
import functools

import jax
import jax.numpy as jnp
from jax import lax
from jax.experimental import pallas as pl
from jax.experimental.pallas import tpu as pltpu
from jax.sharding import PartitionSpec as P


HEAD_DIM = 128
HEADS = 8
KV_HEADS = 2
BLOCK = 128
EXCHANGE_MAX_DEVICES = 16


EPSILON = 1e-06


def exclusive_prefix(state, axis, devices):
    total = jnp.zeros_like(state)
    window = state
    shift = 1
    while shift < devices:
        pairs = [(i, i + shift) for i in range(devices - shift)]
        got = lax.ppermute(window, axis, pairs)
        total = total + got
        if shift * 2 < devices:
            window = window + got
        shift *= 2
    return total


def codes_kernel(pat_ref, pos_ref, codes_ref, *, devices, exchange, nblk, listed, slots):
    pos = pos_ref[0]
    lb = nblk // devices
    for g in range(KV_HEADS):
        for n in range(lb):
            qb = pos * lb + n
            base = (g * lb + n) * slots
            if exchange:
                for c in range(slots):
                    codes_ref[base + c] = jnp.int32(0)
                for j in list(range(1, listed)) + [0]:
                    entry = pat_ref[g, qb, j]
                    owner = entry // lb
                    far_slot = 2 * lb + (pos - owner - 2)
                    near_slot = lb + entry - (pos - 1) * lb
                    own_slot = entry - pos * lb
                    slot = jnp.where(owner == pos, own_slot, jnp.where(owner == pos - 1, near_slot, far_slot))
                    slot = jnp.clip(slot, 0, slots - 1)
                    codes_ref[base + slot] = jnp.int32(2) if j == 0 else jnp.int32(1)
            else:
                codes_ref[base] = jnp.int32(2)
                for c in range(1, slots):
                    entry = pat_ref[g, qb, c]
                    seen = jnp.int32(0)
                    for j in range(c):
                        seen = jnp.where(pat_ref[g, qb, j] == entry, 1, seen)
                    codes_ref[base + c] = 1 - seen


def mask_codes(pattern, position, devices, exchange, slots):
    lb = pattern.shape[1] // devices
    kernel = functools.partial(
        codes_kernel,
        devices=devices,
        exchange=exchange,
        nblk=pattern.shape[1],
        listed=pattern.shape[2],
        slots=slots,
    )
    return pl.pallas_call(
        kernel,
        out_shape=jax.ShapeDtypeStruct((KV_HEADS * lb * slots,), jnp.int32),
        in_specs=[
            pl.BlockSpec(memory_space=pltpu.SMEM),
            pl.BlockSpec(memory_space=pltpu.SMEM),
        ],
        out_specs=pl.BlockSpec(memory_space=pltpu.SMEM),
        cost_estimate=pl.CostEstimate(flops=0, transcendentals=0, bytes_accessed=4 * pattern.size),
    )(pattern, position.reshape(1).astype(jnp.int32))


def attention_kernel(codes_ref, q_ref, *refs, kv_count, shared_table):
    kv_refs = refs[:kv_count]
    o_ref = refs[kv_count]
    table = refs[kv_count + 1]
    g = pl.program_id(0)
    n = pl.program_id(1)
    per_group = o_ref.shape[1] // HEAD_DIM

    def assemble():
        offset = 0
        for ref in kv_refs:
            rows_in = ref.shape[0]
            table[offset:offset + rows_in, :] = ref[...]
            offset += rows_in

    if shared_table:
        pl.when(n == 0)(assemble)
    else:
        assemble()
    keys_total = table.shape[0]
    slots = keys_total // BLOCK
    base = (g * pl.num_programs(1) + n) * slots
    codes = [codes_ref[base + c] for c in range(slots)]
    slot_of_col = lax.broadcasted_iota(jnp.int32, (1, keys_total), 1) // BLOCK
    code = jnp.zeros((1, keys_total), jnp.int32)
    for c in range(slots):
        code = jnp.where(slot_of_col == c, codes[c], code)
    keys = table[:, :HEAD_DIM]
    values = table[:, HEAD_DIM:]
    rows = lax.broadcasted_iota(jnp.int32, (BLOCK, keys_total), 0)
    cols = lax.broadcasted_iota(jnp.int32, (BLOCK, keys_total), 1)
    cols = jnp.bitwise_and(cols, BLOCK - 1)
    allowed = (code == 1) | ((code == 2) & (cols <= rows))
    bias = jnp.where(allowed, 0.0, -jnp.inf)
    scale = HEAD_DIM ** (-0.5)
    for p in range(per_group):
        qp = q_ref[:, p * HEAD_DIM:(p + 1) * HEAD_DIM]
        scores = lax.dot_general(
            qp, keys, (((1,), (1,)), ((), ())), preferred_element_type=jnp.float32
        ) * scale
        scores = scores + bias
        highest = jnp.max(scores, axis=-1, keepdims=True)
        weights = jnp.exp(scores - highest)
        total = jnp.sum(weights, axis=-1, keepdims=True)
        probs = (weights * (1.0 / total)).astype(jnp.bfloat16)
        out = jnp.dot(probs, values, preferred_element_type=jnp.float32)
        o_ref[:, p * HEAD_DIM:(p + 1) * HEAD_DIM] = out.astype(o_ref.dtype)


def kv_spec(piece):
    if piece.ndim == 3:
        return pl.BlockSpec((None, piece.shape[1], 2 * HEAD_DIM), lambda g, n, codes: (g, 0, 0))
    return pl.BlockSpec((None, None, piece.shape[2], 2 * HEAD_DIM), lambda g, n, codes: (g, n, 0, 0))


def attention(soft_query, pieces, pattern, position, devices, exchange):
    tok_count = soft_query.shape[0]
    local_blocks = tok_count // BLOCK
    per_group = HEADS // KV_HEADS
    keys_total = sum(piece.shape[-2] for piece in pieces)
    width = per_group * HEAD_DIM
    flops = 4 * tok_count * HEADS * keys_total * HEAD_DIM
    bytes_accessed = 2 * (2 * soft_query.size + KV_HEADS * local_blocks * keys_total * 2 * HEAD_DIM)
    codes = mask_codes(pattern, position, devices, exchange, keys_total // BLOCK)
    kernel = functools.partial(
        attention_kernel, kv_count=len(pieces), shared_table=all(piece.ndim == 3 for piece in pieces)
    )
    grid_spec = pltpu.PrefetchScalarGridSpec(
        num_scalar_prefetch=1,
        grid=(KV_HEADS, local_blocks),
        in_specs=[pl.BlockSpec((BLOCK, width), lambda g, n, codes: (n, g))]
        + [kv_spec(piece) for piece in pieces],
        out_specs=pl.BlockSpec((BLOCK, width), lambda g, n, codes: (n, g)),
        scratch_shapes=[pltpu.VMEM((keys_total, 2 * HEAD_DIM), jnp.bfloat16)],
    )
    return pl.pallas_call(
        kernel,
        out_shape=jax.ShapeDtypeStruct(soft_query.shape, jnp.bfloat16),
        grid_spec=grid_spec,
        compiler_params=pltpu.CompilerParams(vmem_limit_bytes=48 * 1024 * 1024),
        cost_estimate=pl.CostEstimate(
            flops=flops, transcendentals=tok_count * HEADS * keys_total, bytes_accessed=bytes_accessed
        ),
    )(codes, soft_query, *pieces)


def post_mix_kernel(
    query_ref, key_ref, value_ref, before_ref, lin_gain_ref, lin_out_hbm, hidden_ref,
    soft_gain_ref, wk_hbm, wv_hbm, kv_ref, x_ref, normed_ref, lin_out_ref, wk_ref, wv_ref, sems,
):
    step = pl.program_id(0)
    fetches = [
        pltpu.make_async_copy(lin_out_hbm, lin_out_ref, sems.at[0]),
        pltpu.make_async_copy(wk_hbm, wk_ref, sems.at[1]),
        pltpu.make_async_copy(wv_hbm, wv_ref, sems.at[2]),
    ]

    @pl.when(step == 0)
    def _():
        for fetch in fetches:
            fetch.start()

    per_group = HEADS // KV_HEADS
    rows = lax.broadcasted_iota(jnp.int32, (BLOCK, BLOCK), 0)
    cols = lax.broadcasted_iota(jnp.int32, (BLOCK, BLOCK), 1)
    causal = cols <= rows
    for h in range(HEADS):
        g = h // per_group
        qh = query_ref[:, h * HEAD_DIM:(h + 1) * HEAD_DIM]
        kg = key_ref[:, g * HEAD_DIM:(g + 1) * HEAD_DIM]
        vg = value_ref[:, g * HEAD_DIM:(g + 1) * HEAD_DIM]
        state = before_ref[g]
        high = state.astype(jnp.bfloat16)
        low = (state - high.astype(jnp.float32)).astype(jnp.bfloat16)
        inter = jnp.dot(qh, high, preferred_element_type=jnp.float32)
        inter = inter + jnp.dot(qh, low, preferred_element_type=jnp.float32)
        scores = lax.dot_general(qh, kg, (((1,), (1,)), ((), ())), preferred_element_type=jnp.float32)
        scores = jnp.where(causal, scores, 0.0).astype(jnp.bfloat16)
        intra = jnp.dot(scores, vg, preferred_element_type=jnp.float32)
        part = inter + intra
        power = jnp.mean(part * part, axis=-1, keepdims=True)
        gain = lin_gain_ref[:, h * HEAD_DIM:(h + 1) * HEAD_DIM]
        normed_ref[:, h * HEAD_DIM:(h + 1) * HEAD_DIM] = (
            part * lax.rsqrt(power + EPSILON) * gain
        ).astype(jnp.bfloat16)

    @pl.when(step == 0)
    def _():
        fetches[0].wait()

    branch = jnp.dot(normed_ref[...], lin_out_ref[...], preferred_element_type=jnp.float32)
    residual = (hidden_ref[...].astype(jnp.float32) + branch).astype(jnp.bfloat16)
    widened = residual.astype(jnp.float32)
    power = jnp.mean(widened * widened, axis=-1, keepdims=True)
    layer_in = (widened * lax.rsqrt(power + EPSILON) * soft_gain_ref[...]).astype(jnp.bfloat16)

    @pl.when(step == 0)
    def _():
        fetches[1].wait()
        fetches[2].wait()

    keys = jnp.dot(layer_in, wk_ref[...], preferred_element_type=jnp.float32).astype(jnp.bfloat16)
    values = jnp.dot(layer_in, wv_ref[...], preferred_element_type=jnp.float32).astype(jnp.bfloat16)
    for g in range(KV_HEADS):
        kv_ref[g, :, :HEAD_DIM] = keys[:, g * HEAD_DIM:(g + 1) * HEAD_DIM]
        kv_ref[g, :, HEAD_DIM:] = values[:, g * HEAD_DIM:(g + 1) * HEAD_DIM]
    x_ref[...] = layer_in


def post_mix(lin_query, lin_key, lin_value, before, lin_gain, lin_out_weight, hidden_in, soft_gain, soft_wk, soft_wv):
    tok_count, width = lin_query.shape
    model = hidden_in.shape[1]
    kv_width = lin_key.shape[1]
    steps = tok_count // BLOCK
    whole = lambda i: (0, 0)
    state_spec = pl.BlockSpec((None, KV_HEADS, HEAD_DIM, HEAD_DIM), lambda i: (i, 0, 0, 0))
    flops = 2 * tok_count * (width * model + model * (soft_wk.shape[1] + soft_wv.shape[1]))
    flops += 8 * tok_count * width * HEAD_DIM
    bytes_accessed = 2 * (lin_out_weight.size + hidden_in.size + soft_wk.size + soft_wv.size + lin_query.size)
    return pl.pallas_call(
        post_mix_kernel,
        out_shape=(
            jax.ShapeDtypeStruct((KV_HEADS, tok_count, 2 * HEAD_DIM), jnp.bfloat16),
            jax.ShapeDtypeStruct((tok_count, model), jnp.bfloat16),
        ),
        grid=(steps,),
        in_specs=[
            pl.BlockSpec((BLOCK, width), lambda i: (i, 0)),
            pl.BlockSpec((BLOCK, kv_width), lambda i: (i, 0)),
            pl.BlockSpec((BLOCK, kv_width), lambda i: (i, 0)),
            state_spec,
            pl.BlockSpec((1, width), whole),
            pl.BlockSpec(memory_space=pl.ANY),
            pl.BlockSpec((BLOCK, model), lambda i: (i, 0)),
            pl.BlockSpec((1, model), whole),
            pl.BlockSpec(memory_space=pl.ANY),
            pl.BlockSpec(memory_space=pl.ANY),
        ],
        out_specs=(
            pl.BlockSpec((KV_HEADS, BLOCK, 2 * HEAD_DIM), lambda i: (0, i, 0)),
            pl.BlockSpec((BLOCK, model), lambda i: (i, 0)),
        ),
        scratch_shapes=[
            pltpu.VMEM((BLOCK, width), jnp.bfloat16),
            pltpu.VMEM(lin_out_weight.shape, jnp.bfloat16),
            pltpu.VMEM(soft_wk.shape, jnp.bfloat16),
            pltpu.VMEM(soft_wv.shape, jnp.bfloat16),
            pltpu.SemaphoreType.DMA((3,)),
        ],
        compiler_params=pltpu.CompilerParams(
            vmem_limit_bytes=56 * 1024 * 1024, dimension_semantics=("arbitrary",)
        ),
        cost_estimate=pl.CostEstimate(flops=flops, transcendentals=0, bytes_accessed=bytes_accessed),
    )(
        lin_query,
        lin_key,
        lin_value,
        before,
        lin_gain.reshape(1, -1),
        lin_out_weight,
        hidden_in,
        soft_gain.reshape(1, -1),
        soft_wk,
        soft_wv,
    )


def exchange_kv(per_head, pattern, position, devices):
    tok_count = per_head.shape[1]
    local_blocks = tok_count // BLOCK
    pieces = [per_head]
    if devices > 1:
        pairs = [(i, i + 1) for i in range(devices - 1)]
        pieces.append(lax.ppermute(per_head, "seq", pairs))
    shifts = list(range(2, devices))
    if shifts:
        steps = jnp.array(shifts, jnp.int32)
        far_all = pattern[:, :, 2:].reshape(KV_HEADS, devices, -1)
        on_me = (far_all // local_blocks) == position
        choice_all = jnp.max(jnp.where(on_me, far_all - position * local_blocks, 0), axis=-1)
        dest_ids = jnp.arange(devices, dtype=jnp.int32)
        hit = dest_ids[None, :] == (position + steps)[:, None]
        choice = jnp.sum(jnp.where(hit[:, None, :], choice_all[None], 0), axis=-1)
        split = per_head.reshape(KV_HEADS, local_blocks, BLOCK, 2 * HEAD_DIM)
        chosen = split[None, :, 0]
        for j in range(1, local_blocks):
            chosen = jnp.where((choice == j)[:, :, None, None], split[None, :, j], chosen)
    for i, shift in enumerate(shifts):
        pairs = [(k, k + shift) for k in range(devices - shift)]
        pieces.append(lax.ppermute(chosen[i], "seq", pairs))
    return pieces


def local(
    hidden_in,
    lin_query,
    lin_key,
    lin_value,
    lin_gain,
    lin_out_weight,
    soft_gain,
    soft_wq,
    soft_wk,
    soft_wv,
    pattern,
    *,
    devices,
):
    tok_count = hidden_in.shape[0]
    local_blocks = tok_count // BLOCK
    listed = pattern.shape[2]
    position = lax.axis_index("seq")
    key_blocks = lin_key.reshape(local_blocks, BLOCK, KV_HEADS, HEAD_DIM)
    value_blocks = lin_value.reshape(local_blocks, BLOCK, KV_HEADS, HEAD_DIM)
    block_states = jnp.einsum(
        "ntgd,ntge->ngde", key_blocks, value_blocks, preferred_element_type=jnp.float32
    )
    device_state = jnp.sum(block_states, axis=0)
    carried = exclusive_prefix(device_state, "seq", devices)
    running = jnp.concatenate(
        [jnp.zeros_like(block_states[:1]), jnp.cumsum(block_states[:-1], axis=0)], axis=0
    )
    before = carried[None] + running
    per_head, layer_in = post_mix(
        lin_query, lin_key, lin_value, before, lin_gain, lin_out_weight, hidden_in, soft_gain, soft_wk, soft_wv
    )

    exchange = devices <= EXCHANGE_MAX_DEVICES
    if exchange:
        pieces = exchange_kv(per_head, pattern, position, devices)
    else:
        packed = jnp.transpose(per_head, (1, 0, 2))
        whole = lax.all_gather(packed, "seq", axis=0, tiled=True)
        mine = lax.dynamic_slice_in_dim(pattern, position * local_blocks, local_blocks, 1)
        table = whole.reshape(-1, BLOCK, KV_HEADS, 2 * HEAD_DIM)
        group_ids = jnp.arange(KV_HEADS)[:, None, None]
        tiles = table[mine, :, group_ids, :]
        pieces = [tiles.reshape(KV_HEADS, local_blocks, listed * BLOCK, 2 * HEAD_DIM)]
    soft_query = jnp.dot(layer_in, soft_wq, preferred_element_type=jnp.float32).astype(jnp.bfloat16)
    return attention(soft_query, pieces, pattern, position, devices, exchange)


def solution(mesh):
    in_specs = (
        P(("dp", "seq"), None),
        P(("dp", "seq"), None),
        P(("dp", "seq"), None),
        P(("dp", "seq"), None),
        P(),
        P(),
        P(),
        P(),
        P(),
        P(),
        P(),
    )
    out_specs = P(("dp", "seq"), None)
    devices = mesh.shape["seq"]
    body = functools.partial(local, devices=devices)
    return jax.shard_map(body, mesh=mesh, in_specs=in_specs, out_specs=out_specs, check_vma=False)
```
